128 devices in a mesh: tod: 16 (over z, x), map: 8 (over y, core).
Axes of the slice: x: 4, y: 4, z: 4, core: 2. Of those that a mesh axis runs over, the one named last changes fastest.
Arguments:
- tod: float32 [128, 65536], P('map', 'tod'), may hold values from -6 to 6
- det_angle: float32 [128], P('map'), may hold values from -3.140625 to 3.140625
- angle_index: int32 [128, 65536], P('map', 'tod'), may hold values from 0 to 63
- offsets: int32 [128, 65536], P('map', 'tod'), may hold values from 0 to 255
- block_slot: int32 [128, 256], P('map', 'tod'), may hold values from 0 to 255, as said below
- hit_tiles: int32 [128, 128, 2], P(('tod', 'map')), may hold values from -1 to 383, as said below
- noise_filter: float32 [128, 129], P('map'), may hold values from -0.9 to 2, as said below
- precond: float32 [49152, 6, 256], P(('tod', 'map')), may hold values from -0.45 to 1, as said below
Outputs:
- solution: float32 [49152, 3, 256], P(('tod', 'map'))
- residual: float32 [49152, 3, 256], P(('tod', 'map'))
The draws below stay inside these ranges and needn't reach their ends.
Inputs may be any that keep to these rules, and one draw needn't show every extreme that they name: `hit_tiles`: entry [g, o, j] is slot j of owner o's tiles touched by shard g, a tile index within the owner's 384 tiles, or -1 for an empty slot; used slots come first in a row and hold distinct tiles; some owner has all 2 slots used from every shard. `block_slot`: each entry h names a used slot, hit_tiles[g, h // 2, h % 2] >= 0, of the shard g that holds the block. `noise_filter`: each row defines a symmetric positive definite Toeplitz filter. `precond`: each pixel's 3x3 block is symmetric positive definite.
All inputs are finite; a program needn't handle non-finite values.
Results may differ from the reference program's by a relative error of at most 0.00028.
Values sent between devices are 32-bit elements; how exact they have to be, the bound alone decides.
No kernel may reach another device: no remote copies, remote signals or barrier semaphores. Data moves between devices by JAX's collectives and lax.ppermute only.
A program may use at most 64 MiB of HBM per device.

```python
import jax
import jax.numpy as jnp
from jax import lax

TILE = 256
TILES_DEV = 384
SLOT = 2
DET_DEV = 16
SAMP_DEV = 4096
BLOCK = 256
BAND = 128
ANGLES = 64
ITERS = 2
SHARDS = 128
DETS = 128
NSAMP = 65536
NBLOCKS = 256
HIT = 256
TILES = 49152


def hit_table(key):
    key_used, key_full, key_tiles = jax.random.split(jax.random.fold_in(key, 7), 3)
    used = jax.random.randint(key_used, (SHARDS, SHARDS), 0, SLOT + 1)
    full = jax.random.randint(key_full, (), 0, SHARDS)
    used = jnp.where(jnp.arange(SHARDS)[None, :] == full, SLOT, used)
    keys = jax.random.split(key_tiles, SHARDS * SHARDS)
    picks = jax.vmap(lambda one: jax.random.permutation(one, TILES_DEV)[:SLOT])(keys)
    picks = picks.reshape(SHARDS, SHARDS, SLOT)
    valid = jnp.arange(SLOT)[None, None, :] < used[:, :, None]
    return (jnp.where(valid, picks, -1).astype(jnp.int32), valid)


def draw_hit_tiles(key, part):
    tiles, valid = hit_table(key)
    return tiles


def draw_block_slot(key, part):
    tiles, valid = hit_table(key)
    flat_valid = valid.reshape(SHARDS, HIT)
    ranks = jnp.cumsum(flat_valid.astype(jnp.int32), axis=1) - 1
    counts = jnp.sum(flat_valid.astype(jnp.int32), axis=1)
    det = jnp.arange(DETS)[:, None]
    blk = jnp.arange(NBLOCKS)[None, :]
    group = blk // (SAMP_DEV // BLOCK) * (DETS // DET_DEV) + det // DET_DEV
    pick = jax.random.randint(jax.random.fold_in(key, 9), (DETS, NBLOCKS), 0, 2 ** 30) % counts[group]
    match = flat_valid[group] & (ranks[group] == pick[:, :, None])
    return jnp.argmax(match, axis=2).astype(jnp.int32)


def draw_noise_filter(key, part):
    key_centre, key_side = jax.random.split(jax.random.fold_in(key, 3))
    centre = jnp.exp(jax.random.uniform(key_centre, (DETS, 1), jnp.float32, jnp.log(0.5), jnp.log(2.0)))
    lags = jnp.arange(1, BAND + 1).astype(jnp.float32)
    spread = jax.random.uniform(key_side, (DETS, BAND), jnp.float32, 0.2, 1.0)
    shape = spread * lags[None, :] ** (-0.5)
    side = -0.45 * centre * shape / jnp.sum(shape, axis=1, keepdims=True)
    return jnp.concatenate([centre, side], axis=1).astype(jnp.float32)


def draw_precond(key, part):
    key_diag, key_size, key_sign = jax.random.split(jax.random.fold_in(key, 5), 3)
    low = jnp.log(0.1)
    diag = jnp.exp(jax.random.uniform(key_diag, (TILES, 3, TILE), jnp.float32, low, 0.0))
    size = jax.random.uniform(key_size, (TILES, 3, TILE), jnp.float32, 0.15, 0.45)
    signs = (jax.random.randint(key_sign, (TILES, 3, TILE), 0, 2) * 2 - 1).astype(jnp.float32)
    cross_iq = signs[:, 0] * size[:, 0] * jnp.sqrt(diag[:, 0] * diag[:, 1])
    cross_iu = signs[:, 1] * size[:, 1] * jnp.sqrt(diag[:, 0] * diag[:, 2])
    cross_qu = signs[:, 2] * size[:, 2] * jnp.sqrt(diag[:, 1] * diag[:, 2])
    cross = jnp.stack([cross_iq, cross_iu, cross_qu], axis=1)
    return jnp.concatenate([diag, cross], axis=1).astype(jnp.float32)


def touch_ends(values, stream_key, smallest, top_value):
    index_at = [jax.random.randint(jax.random.fold_in(stream_key, axis), (), 0, length) for axis, length in enumerate(values.shape)]
    main_axis = values.shape.index(max(values.shape))
    neighbour = index_at[:main_axis] + [(index_at[main_axis] + 1) % values.shape[main_axis]] + index_at[main_axis + 1:]
    return values.at[tuple(index_at)].set(smallest).at[tuple(neighbour)].set(top_value)


def level_of(key, dims, cuts, smallest, top_value):
    def one(dim, shards_of):
        steps = jax.random.uniform(jax.random.fold_in(jax.random.fold_in(key, 6), dim), (shards_of,), jnp.float32, smallest / len(cuts), top_value / len(cuts))
        return jnp.repeat(jnp.exp(steps), dims[dim] // shards_of).reshape((-1,) + (1,) * (len(dims) - dim - 1))

    loudness = one(*cuts[0])
    for cut in cuts[1:]:
        loudness = loudness * one(*cut)
    return loudness


def noise(own_key, shape, scale, reach, cuts=(), kind=jnp.bfloat16):
    drawn = jax.random.normal(own_key, shape, jnp.float32) * scale
    if len(cuts) > 0:
        drawn = level_of(own_key, shape, cuts, -0.22, 0.18) * drawn
    return jnp.clip(drawn, min=-reach, max=reach).astype(kind)


def setup_inputs(seed: int = 0) -> dict:
    splits = jax.random.split(jax.random.key(seed), 9)
    return {
        "tod": noise(splits[0], (DETS, NSAMP), 1.0, 6.0, ((0, 8), (1, 16)), jnp.float32),
        "det_angle": jnp.clip(jax.random.uniform(splits[1], (DETS,), jnp.float32, -3.140625, 3.140625), -3.140625, 3.140625),
        "angle_index": touch_ends(jax.random.randint(splits[2], (DETS, NSAMP), 0, ANGLES), jax.random.fold_in(splits[2], 1), 0, ANGLES - 1).astype(jnp.int32),
        "offsets": touch_ends(jax.random.randint(splits[3], (DETS, NSAMP), 0, TILE), jax.random.fold_in(splits[3], 1), 0, TILE - 1).astype(jnp.int32),
        "block_slot": draw_block_slot(jax.random.fold_in(splits[8], 71), 0),
        "hit_tiles": draw_hit_tiles(jax.random.fold_in(splits[8], 71), 0),
        "noise_filter": draw_noise_filter(jax.random.fold_in(splits[8], 71), 0),
        "precond": draw_precond(jax.random.fold_in(splits[8], 71), 0),
    }


def sample_index(hit_tiles, block_slot, offsets):
    det = jnp.arange(DETS, dtype=jnp.int32)[:, None]
    blk = jnp.arange(NBLOCKS, dtype=jnp.int32)[None, :]
    group = (blk // (SAMP_DEV // BLOCK)) * (DETS // DET_DEV) + det // DET_DEV
    owner = block_slot // SLOT
    slot = block_slot % SLOT
    tile = owner * TILES_DEV + hit_tiles[group, owner, slot]
    tile = jnp.repeat(tile, BLOCK, axis=1)
    return (tile * (3 * TILE) + offsets).astype(jnp.int32)


def project(field, index, cosine, sine):
    flat = field.reshape(-1)
    return flat[index] + cosine * flat[index + TILE] + sine * flat[index + 2 * TILE]


def binning(values, index, cosine, sine):
    total = jnp.zeros((TILES * 3 * TILE,), values.dtype)
    total = total.at[index].add(values)
    total = total.at[index + TILE].add(cosine * values)
    total = total.at[index + 2 * TILE].add(sine * values)
    return total.reshape(TILES, 3, TILE)


def noise_weight(stream, taps):
    padded = jnp.pad(stream, ((0, 0), (BAND, BAND)))

    def add_lag(lag, total):
        ahead = lax.dynamic_slice_in_dim(padded, BAND + lag, NSAMP, 1)
        behind = lax.dynamic_slice_in_dim(padded, BAND - lag, NSAMP, 1)
        weight = lax.dynamic_slice_in_dim(taps, lag, 1, 1)
        return total + weight * (ahead + behind)

    return lax.fori_loop(1, BAND + 1, add_lag, taps[:, :1] * stream)


def precondition(field, precond):
    first, second, third = field[:, 0], field[:, 1], field[:, 2]
    row_one = precond[:, 0] * first + precond[:, 3] * second + precond[:, 4] * third
    row_two = precond[:, 3] * first + precond[:, 1] * second + precond[:, 5] * third
    row_three = precond[:, 4] * first + precond[:, 5] * second + precond[:, 2] * third
    return jnp.stack([row_one, row_two, row_three], axis=1)


def reference(tod, det_angle, angle_index, offsets, block_slot, hit_tiles, noise_filter, precond):
    index = sample_index(hit_tiles, block_slot, offsets)
    psi = det_angle[:, None] + jnp.pi * angle_index.astype(jnp.float32) / ANGLES
    cosine = jnp.cos(2.0 * psi)
    sine = jnp.sin(2.0 * psi)

    def operator(field):
        return binning(noise_weight(project(field, index, cosine, sine), noise_filter), index, cosine, sine)

    rhs = binning(noise_weight(tod, noise_filter), index, cosine, sine)
    solution = jnp.zeros_like(rhs)
    residual = rhs
    zeta = precondition(residual, precond)
    direction = zeta
    norm_now = jnp.sum(residual * zeta)
    for step in range(ITERS):
        image = operator(direction)
        alpha = norm_now / jnp.sum(direction * image)
        solution = solution + alpha * direction
        residual = residual - alpha * image
        if step + 1 < ITERS:
            zeta = precondition(residual, precond)
            norm_next = jnp.sum(residual * zeta)
            direction = zeta + (norm_next / norm_now) * direction
            norm_now = norm_next
    return solution, residual
```

```python
import jax
import jax.numpy as jnp
from jax import lax
from jax.sharding import PartitionSpec as P

ANGLES = 64
ITERS = 2
SIDE = 128


def extended(cells, sides, width):
    for axis, dim in sides:
        count = lax.axis_size(axis)
        ends = count - 1
        head = lax.slice_in_dim(cells, 0, width, axis=dim)
        tail = lax.slice_in_dim(cells, cells.shape[dim] - width, cells.shape[dim], axis=dim)
        cells = jnp.concatenate(
            [
                lax.ppermute(tail, axis, [(i, (i + 1) % count) for i in range(ends)]),
                cells,
                lax.ppermute(head, axis, [((i + 1) % count, i) for i in range(ends)]),
            ],
            axis=dim,
        )
    return cells


def precondition(field, precond):
    first, second, third = (field[:, 0], field[:, 1], field[:, 2])
    row_one = precond[:, 0] * first + precond[:, 3] * second + precond[:, 4] * third
    row_two = precond[:, 3] * first + precond[:, 1] * second + precond[:, 5] * third
    row_three = precond[:, 4] * first + precond[:, 5] * second + precond[:, 2] * third
    return jnp.stack([row_one, row_two, row_three], axis=1)


def exchange(rows, partial):
    shards = rows.shape[0]
    if partial is not None:
        extra = jnp.broadcast_to(partial.astype(jnp.float32), (shards, SIDE))
        rows = jnp.concatenate([rows, extra], axis=1)
    got = lax.all_to_all(rows, ("tod", "map"), split_axis=0, concat_axis=0, tiled=True)
    if partial is None:
        return got, None
    width = got.shape[1] - SIDE
    return got[:, :width], jnp.sum(got[:, width])


def local(tod, det_angle, angle_index, offsets, block_slot, hit_tiles, noise_filter, precond):
    shards = lax.axis_size(("tod", "map"))
    hits = hit_tiles[0]
    slot_count = hits.shape[1]
    owner_lists = lax.all_to_all(hits, ("tod", "map"), split_axis=0, concat_axis=0, tiled=True)
    tiles_dev = precond.shape[0]
    tile_pix = precond.shape[2]
    det_count, samp_count = tod.shape
    blocks_per_det = block_slot.shape[1]
    block_len = samp_count // blocks_per_det
    block_total = det_count * blocks_per_det
    hit_total = shards * slot_count
    split = 16
    while split * split < tile_pix:
        split *= 2
    low_count = tile_pix // split
    highest = lax.Precision.HIGHEST
    choose = (
        block_slot.reshape(-1)[:, None] == jnp.arange(hit_total, dtype=jnp.int32)[None, :]
    ).astype(jnp.float32)
    psi = det_angle[:, None] + jnp.pi * angle_index.astype(jnp.float32) / ANGLES
    stokes = jnp.stack([jnp.ones_like(psi), jnp.cos(2.0 * psi), jnp.sin(2.0 * psi)], axis=1)
    stokes_b = (
        stokes.reshape(det_count, 3, blocks_per_det, block_len)
        .transpose(0, 2, 1, 3)
        .reshape(block_total, 3, block_len)
    )
    placement = (
        owner_lists.reshape(-1)[:, None] == jnp.arange(tiles_dev, dtype=jnp.int32)[None, :]
    ).astype(jnp.float32)
    offs_b = offsets.reshape(block_total, block_len)
    high_hot = (
        (offs_b // low_count)[:, None, :] == jnp.arange(split, dtype=jnp.int32)[None, :, None]
    ).astype(jnp.float32)
    low_hot = (
        (offs_b % low_count)[:, None, :] == jnp.arange(low_count, dtype=jnp.int32)[None, :, None]
    ).astype(jnp.float32)

    band = noise_filter.shape[1] - 1
    width = 2 * band
    rows = jnp.arange(2 * width, dtype=jnp.int32)[:, None]
    cols = jnp.arange(width, dtype=jnp.int32)[None, :]
    lag = jnp.abs(rows - cols - band)
    lag_hot = (lag[:, :, None] == jnp.arange(band + 1, dtype=jnp.int32)[None, None, :]).astype(
        jnp.float32
    )
    toeplitz = jnp.einsum(
        "dk,rck->drc", noise_filter, lag_hot, precision=highest, preferred_element_type=jnp.float32
    )

    def weigh(stream):
        padded = extended(stream, (("tod", 1),), band)
        head = padded[:, :samp_count].reshape(det_count, -1, width)
        tail = padded[:, width:].reshape(det_count, -1, width)
        out = jnp.einsum(
            "dbj,dji->dbi",
            head,
            toeplitz[:, :width],
            precision=highest,
            preferred_element_type=jnp.float32,
        )
        out = out + jnp.einsum(
            "dbj,dji->dbi",
            tail,
            toeplitz[:, width:],
            precision=highest,
            preferred_element_type=jnp.float32,
        )
        return out.reshape(det_count, samp_count)

    def binning(stream, partial):
        values = stokes_b * stream.reshape(block_total, 1, block_len)
        spread = values[:, :, None, :] * high_hot[:, None, :, :]
        block_maps = jnp.einsum(
            "bsan,bcn->bsac",
            spread,
            low_hot,
            precision=highest,
            preferred_element_type=jnp.float32,
        ).reshape(block_total, 3 * tile_pix)
        touched = lax.dot_general(
            choose,
            block_maps,
            (((0,), (0,)), ((), ())),
            precision=highest,
            preferred_element_type=jnp.float32,
        )
        arrived, total = exchange(touched.reshape(shards, slot_count * 3 * tile_pix), partial)
        summed = lax.dot_general(
            placement,
            arrived.reshape(hit_total, 3 * tile_pix),
            (((0,), (0,)), ((), ())),
            precision=highest,
            preferred_element_type=jnp.float32,
        )
        return summed.reshape(tiles_dev, 3, tile_pix), total

    def projection(field, partial):
        outgoing = jnp.dot(
            placement,
            field.reshape(tiles_dev, 3 * tile_pix),
            precision=highest,
            preferred_element_type=jnp.float32,
        )
        touched, total = exchange(outgoing.reshape(shards, slot_count * 3 * tile_pix), partial)
        block_maps = jnp.dot(
            choose,
            touched.reshape(hit_total, 3 * tile_pix),
            precision=highest,
            preferred_element_type=jnp.float32,
        ).reshape(block_total, 3, split, low_count)
        partly = jnp.einsum(
            "bsac,bcn->bsan",
            block_maps,
            low_hot,
            precision=highest,
            preferred_element_type=jnp.float32,
        )
        values = jnp.sum(partly * high_hot[:, None, :, :], axis=2)
        stream = jnp.sum(values * stokes_b, axis=1)
        return stream.reshape(det_count, samp_count), total

    rhs, _ = binning(weigh(tod), None)
    solution = jnp.zeros_like(rhs)
    residual = rhs
    zeta = precondition(residual, precond)
    direction = zeta
    stream_dir, norm_now = projection(zeta, jnp.sum(residual * zeta))
    for step in range(ITERS):
        weighed = weigh(stream_dir)
        image, curvature = binning(weighed, jnp.sum(stream_dir * weighed))
        alpha = norm_now / curvature
        solution = solution + alpha * direction
        residual = residual - alpha * image
        if step + 1 < ITERS:
            zeta = precondition(residual, precond)
            stream_zeta, norm_next = projection(zeta, jnp.sum(residual * zeta))
            beta = norm_next / norm_now
            direction = zeta + beta * direction
            stream_dir = stream_zeta + beta * stream_dir
            norm_now = norm_next
    return (solution, residual)


def solution(mesh):
    in_specs = (
        P("map", "tod"),
        P("map"),
        P("map", "tod"),
        P("map", "tod"),
        P("map", "tod"),
        P(("tod", "map"), None, None),
        P("map", None),
        P(("tod", "map"), None, None),
    )
    out_specs = (P(("tod", "map"), None, None), P(("tod", "map"), None, None))
    return jax.shard_map(local, mesh=mesh, in_specs=in_specs, out_specs=out_specs, check_vma=False)
```

```python
import jax
import jax.numpy as jnp
from jax import lax
from jax.sharding import PartitionSpec as P

ANGLES = 64
ITERS = 2
SIDE = 128


def extended(cells, sides, width):
    for axis, dim in sides:
        count = lax.axis_size(axis)
        ends = count - 1
        head = lax.slice_in_dim(cells, 0, width, axis=dim)
        tail = lax.slice_in_dim(cells, cells.shape[dim] - width, cells.shape[dim], axis=dim)
        cells = jnp.concatenate(
            [
                lax.ppermute(tail, axis, [(i, (i + 1) % count) for i in range(ends)]),
                cells,
                lax.ppermute(head, axis, [((i + 1) % count, i) for i in range(ends)]),
            ],
            axis=dim,
        )
    return cells


def precondition(field, precond):
    first, second, third = (field[:, 0], field[:, 1], field[:, 2])
    row_one = precond[:, 0] * first + precond[:, 3] * second + precond[:, 4] * third
    row_two = precond[:, 3] * first + precond[:, 1] * second + precond[:, 5] * third
    row_three = precond[:, 4] * first + precond[:, 5] * second + precond[:, 2] * third
    return jnp.stack([row_one, row_two, row_three], axis=1)


def exchange(rows, partial):
    shards = rows.shape[0]
    if partial is not None:
        extra = jnp.broadcast_to(partial.astype(jnp.float32), (shards, SIDE))
        rows = jnp.concatenate([rows, extra], axis=1)
    got = lax.all_to_all(rows, ("tod", "map"), split_axis=0, concat_axis=0, tiled=True)
    if partial is None:
        return got, None
    width = got.shape[1] - SIDE
    return got[:, :width], jnp.sum(got[:, width])


def local(tod, det_angle, angle_index, offsets, block_slot, hit_tiles, noise_filter, precond):
    shards = lax.axis_size(("tod", "map"))
    hits = hit_tiles[0]
    slot_count = hits.shape[1]
    owner_lists = lax.all_to_all(hits, ("tod", "map"), split_axis=0, concat_axis=0, tiled=True)
    tiles_dev = precond.shape[0]
    tile_pix = precond.shape[2]
    det_count, samp_count = tod.shape
    blocks_per_det = block_slot.shape[1]
    block_len = samp_count // blocks_per_det
    block_total = det_count * blocks_per_det
    hit_total = shards * slot_count
    split = 16
    while split * split < tile_pix:
        split *= 2
    low_count = tile_pix // split
    highest = lax.Precision.HIGH
    choose = (
        block_slot.reshape(-1)[:, None] == jnp.arange(hit_total, dtype=jnp.int32)[None, :]
    ).astype(jnp.float32)
    psi = det_angle[:, None] + jnp.pi * angle_index.astype(jnp.float32) / ANGLES
    stokes = jnp.stack([jnp.ones_like(psi), jnp.cos(2.0 * psi), jnp.sin(2.0 * psi)], axis=1)
    stokes_b = (
        stokes.reshape(det_count, 3, blocks_per_det, block_len)
        .transpose(0, 2, 1, 3)
        .reshape(block_total, 3, block_len)
    )
    placement = (
        owner_lists.reshape(-1)[:, None] == jnp.arange(tiles_dev, dtype=jnp.int32)[None, :]
    ).astype(jnp.float32)
    owner_flat = owner_lists.reshape(-1)
    owner_index = jnp.clip(owner_flat, 0, tiles_dev - 1)
    offs_b = offsets.reshape(block_total, block_len)
    high_hot = (
        (offs_b // low_count)[:, None, :] == jnp.arange(split, dtype=jnp.int32)[None, :, None]
    ).astype(jnp.float32)
    low_hot = (
        (offs_b % low_count)[:, None, :] == jnp.arange(low_count, dtype=jnp.int32)[None, :, None]
    ).astype(jnp.float32)

    band = noise_filter.shape[1] - 1
    width = 2 * band
    rows = jnp.arange(2 * width, dtype=jnp.int32)[:, None]
    cols = jnp.arange(width, dtype=jnp.int32)[None, :]
    lag = jnp.abs(rows - cols - band)
    lag_hot = (lag[:, :, None] == jnp.arange(band + 1, dtype=jnp.int32)[None, None, :]).astype(
        jnp.float32
    )
    toeplitz = jnp.einsum(
        "dk,rck->drc", noise_filter, lag_hot, precision=highest, preferred_element_type=jnp.float32
    )

    def weigh(stream):
        padded = extended(stream, (("tod", 1),), band)
        head = padded[:, :samp_count].reshape(det_count, -1, width)
        tail = padded[:, width:].reshape(det_count, -1, width)
        out = jnp.einsum(
            "dbj,dji->dbi",
            head,
            toeplitz[:, :width],
            precision=highest,
            preferred_element_type=jnp.float32,
        )
        out = out + jnp.einsum(
            "dbj,dji->dbi",
            tail,
            toeplitz[:, width:],
            precision=highest,
            preferred_element_type=jnp.float32,
        )
        return out.reshape(det_count, samp_count)

    def binning(stream, partial):
        values = stokes_b * stream.reshape(block_total, 1, block_len)
        spread = values[:, :, None, :] * high_hot[:, None, :, :]
        block_maps = jnp.einsum(
            "bsan,bcn->bsac",
            spread,
            low_hot,
            precision=highest,
            preferred_element_type=jnp.float32,
        ).reshape(block_total, 3 * tile_pix)
        touched = lax.dot_general(
            choose,
            block_maps,
            (((0,), (0,)), ((), ())),
            precision=highest,
            preferred_element_type=jnp.float32,
        )
        arrived, total = exchange(touched.reshape(shards, slot_count * 3 * tile_pix), partial)
        summed = lax.dot_general(
            placement,
            arrived.reshape(hit_total, 3 * tile_pix),
            (((0,), (0,)), ((), ())),
            precision=highest,
            preferred_element_type=jnp.float32,
        )
        return summed.reshape(tiles_dev, 3, tile_pix), total

    def projection(field, partial):
        outgoing = jnp.where(
            (owner_flat >= 0)[:, None],
            jnp.take(field.reshape(tiles_dev, 3 * tile_pix), owner_index, axis=0),
            0.0,
        )
        touched, total = exchange(outgoing.reshape(shards, slot_count * 3 * tile_pix), partial)
        block_maps = jnp.take(
            touched.reshape(hit_total, 3 * tile_pix), block_slot.reshape(-1), axis=0
        ).reshape(block_total, 3, split, low_count)
        partly = jnp.einsum(
            "bsac,bcn->bsan",
            block_maps,
            low_hot,
            precision=highest,
            preferred_element_type=jnp.float32,
        )
        values = jnp.sum(partly * high_hot[:, None, :, :], axis=2)
        stream = jnp.sum(values * stokes_b, axis=1)
        return stream.reshape(det_count, samp_count), total

    rhs, _ = binning(weigh(tod), None)
    solution = jnp.zeros_like(rhs)
    residual = rhs
    zeta = precondition(residual, precond)
    direction = zeta
    stream_dir, norm_now = projection(zeta, jnp.sum(residual * zeta))
    for step in range(ITERS):
        weighed = weigh(stream_dir)
        image, curvature = binning(weighed, jnp.sum(stream_dir * weighed))
        alpha = norm_now / curvature
        solution = solution + alpha * direction
        residual = residual - alpha * image
        if step + 1 < ITERS:
            zeta = precondition(residual, precond)
            stream_zeta, norm_next = projection(zeta, jnp.sum(residual * zeta))
            beta = norm_next / norm_now
            direction = zeta + beta * direction
            stream_dir = stream_zeta + beta * stream_dir
            norm_now = norm_next
    return (solution, residual)


def solution(mesh):
    in_specs = (
        P("map", "tod"),
        P("map"),
        P("map", "tod"),
        P("map", "tod"),
        P("map", "tod"),
        P(("tod", "map"), None, None),
        P("map", None),
        P(("tod", "map"), None, None),
    )
    out_specs = (P(("tod", "map"), None, None), P(("tod", "map"), None, None))
    return jax.shard_map(local, mesh=mesh, in_specs=in_specs, out_specs=out_specs, check_vma=False)
```

```python
import jax
import jax.numpy as jnp
from jax import lax
from jax.sharding import PartitionSpec as P

ANGLES = 64
ITERS = 2
SIDE = 128


def extended(cells, sides, width):
    for axis, dim in sides:
        count = lax.axis_size(axis)
        ends = count - 1
        head = lax.slice_in_dim(cells, 0, width, axis=dim)
        tail = lax.slice_in_dim(cells, cells.shape[dim] - width, cells.shape[dim], axis=dim)
        cells = jnp.concatenate(
            [
                lax.ppermute(tail, axis, [(i, (i + 1) % count) for i in range(ends)]),
                cells,
                lax.ppermute(head, axis, [((i + 1) % count, i) for i in range(ends)]),
            ],
            axis=dim,
        )
    return cells


def precondition(field, precond):
    first, second, third = (field[:, 0], field[:, 1], field[:, 2])
    row_one = precond[:, 0] * first + precond[:, 3] * second + precond[:, 4] * third
    row_two = precond[:, 3] * first + precond[:, 1] * second + precond[:, 5] * third
    row_three = precond[:, 4] * first + precond[:, 5] * second + precond[:, 2] * third
    return jnp.stack([row_one, row_two, row_three], axis=1)


def exchange(rows, partial):
    shards = rows.shape[0]
    if partial is not None:
        extra = jnp.broadcast_to(partial.astype(jnp.float32), (shards, SIDE))
        rows = jnp.concatenate([rows, extra], axis=1)
    got = lax.all_to_all(rows, ("tod", "map"), split_axis=0, concat_axis=0, tiled=True)
    if partial is None:
        return got, None
    width = got.shape[1] - SIDE
    return got[:, :width], jnp.sum(got[:, width])


def local(tod, det_angle, angle_index, offsets, block_slot, hit_tiles, noise_filter, precond):
    shards = lax.axis_size(("tod", "map"))
    hits = hit_tiles[0]
    slot_count = hits.shape[1]
    owner_lists = lax.all_to_all(hits, ("tod", "map"), split_axis=0, concat_axis=0, tiled=True)
    tiles_dev = precond.shape[0]
    tile_pix = precond.shape[2]
    det_count, samp_count = tod.shape
    blocks_per_det = block_slot.shape[1]
    block_len = samp_count // blocks_per_det
    block_total = det_count * blocks_per_det
    hit_total = shards * slot_count
    split = 16
    while split * split < tile_pix:
        split *= 2
    low_count = tile_pix // split
    highest = lax.Precision.HIGH
    psi = det_angle[:, None] + jnp.pi * angle_index.astype(jnp.float32) / ANGLES
    stokes = jnp.stack([jnp.ones_like(psi), jnp.cos(2.0 * psi), jnp.sin(2.0 * psi)], axis=1)
    stokes_b = (
        stokes.reshape(det_count, 3, blocks_per_det, block_len)
        .transpose(0, 2, 1, 3)
        .reshape(block_total, 3, block_len)
    )
    placement = (
        owner_lists.reshape(-1)[:, None] == jnp.arange(tiles_dev, dtype=jnp.int32)[None, :]
    ).astype(jnp.float32)
    owner_flat = owner_lists.reshape(-1)
    owner_index = jnp.clip(owner_flat, 0, tiles_dev - 1)
    offs_b = offsets.reshape(block_total, block_len)
    high_hot = (
        (offs_b // low_count)[:, None, :] == jnp.arange(split, dtype=jnp.int32)[None, :, None]
    ).astype(jnp.float32)
    low_hot = (
        (offs_b % low_count)[:, None, :] == jnp.arange(low_count, dtype=jnp.int32)[None, :, None]
    ).astype(jnp.float32)

    band = noise_filter.shape[1] - 1
    rows = jnp.arange(3 * band, dtype=jnp.int32)[:, None]
    cols = jnp.arange(band, dtype=jnp.int32)[None, :]
    lag = jnp.abs(rows - cols - band)
    lag_hot = (lag[:, :, None] == jnp.arange(band + 1, dtype=jnp.int32)[None, None, :]).astype(
        jnp.float32
    )
    toeplitz = jnp.einsum(
        "dk,rck->drc", noise_filter, lag_hot, precision=highest, preferred_element_type=jnp.float32
    )
    block_count = samp_count // band

    def weigh(stream):
        padded = extended(stream, (("tod", 1),), band).reshape(det_count, block_count + 2, band)
        stacked = jnp.concatenate(
            [padded[:, k : k + block_count] for k in range(3)], axis=2
        )
        out = jnp.einsum(
            "dbj,dji->dbi",
            stacked,
            toeplitz,
            precision=highest,
            preferred_element_type=jnp.float32,
        )
        return out.reshape(det_count, samp_count)

    def binning(stream, partial):
        values = stokes_b * stream.reshape(block_total, 1, block_len)
        spread = values[:, :, None, :] * high_hot[:, None, :, :]
        block_maps = jnp.einsum(
            "bsan,bcn->bsac",
            spread,
            low_hot,
            precision=highest,
            preferred_element_type=jnp.float32,
        ).reshape(block_total, 3 * tile_pix)
        touched = jnp.zeros((hit_total, 3 * tile_pix), jnp.float32).at[block_slot.reshape(-1)].add(
            block_maps
        )
        arrived, total = exchange(touched.reshape(shards, slot_count * 3 * tile_pix), partial)
        summed = lax.dot_general(
            placement,
            arrived.reshape(hit_total, 3 * tile_pix),
            (((0,), (0,)), ((), ())),
            precision=highest,
            preferred_element_type=jnp.float32,
        )
        return summed.reshape(tiles_dev, 3, tile_pix), total

    def projection(field, partial):
        outgoing = jnp.where(
            (owner_flat >= 0)[:, None],
            jnp.take(field.reshape(tiles_dev, 3 * tile_pix), owner_index, axis=0),
            0.0,
        )
        touched, total = exchange(outgoing.reshape(shards, slot_count * 3 * tile_pix), partial)
        block_maps = jnp.take(
            touched.reshape(hit_total, 3 * tile_pix), block_slot.reshape(-1), axis=0
        ).reshape(block_total, 3, split, low_count)
        partly = jnp.einsum(
            "bsac,bcn->bsan",
            block_maps,
            low_hot,
            precision=highest,
            preferred_element_type=jnp.float32,
        )
        values = jnp.sum(partly * high_hot[:, None, :, :], axis=2)
        stream = jnp.sum(values * stokes_b, axis=1)
        return stream.reshape(det_count, samp_count), total

    rhs, _ = binning(weigh(tod), None)
    solution = jnp.zeros_like(rhs)
    residual = rhs
    zeta = precondition(residual, precond)
    direction = zeta
    stream_dir, norm_now = projection(zeta, jnp.sum(residual * zeta))
    for step in range(ITERS):
        weighed = weigh(stream_dir)
        image, curvature = binning(weighed, jnp.sum(stream_dir * weighed))
        alpha = norm_now / curvature
        solution = solution + alpha * direction
        residual = residual - alpha * image
        if step + 1 < ITERS:
            zeta = precondition(residual, precond)
            stream_zeta, norm_next = projection(zeta, jnp.sum(residual * zeta))
            beta = norm_next / norm_now
            direction = zeta + beta * direction
            stream_dir = stream_zeta + beta * stream_dir
            norm_now = norm_next
    return (solution, residual)


def solution(mesh):
    in_specs = (
        P("map", "tod"),
        P("map"),
        P("map", "tod"),
        P("map", "tod"),
        P("map", "tod"),
        P(("tod", "map"), None, None),
        P("map", None),
        P(("tod", "map"), None, None),
    )
    out_specs = (P(("tod", "map"), None, None), P(("tod", "map"), None, None))
    return jax.shard_map(local, mesh=mesh, in_specs=in_specs, out_specs=out_specs, check_vma=False)
```

```python
import jax
import jax.numpy as jnp
from jax import lax
from jax.experimental import pallas as pl
from jax.experimental.pallas import tpu as pltpu
from jax.sharding import PartitionSpec as P

ANGLES = 64
ITERS = 2
SIDE = 128


def extended(cells, sides, width):
    for axis, dim in sides:
        count = lax.axis_size(axis)
        ends = count - 1
        head = lax.slice_in_dim(cells, 0, width, axis=dim)
        tail = lax.slice_in_dim(cells, cells.shape[dim] - width, cells.shape[dim], axis=dim)
        cells = jnp.concatenate(
            [
                lax.ppermute(tail, axis, [(i, (i + 1) % count) for i in range(ends)]),
                cells,
                lax.ppermute(head, axis, [((i + 1) % count, i) for i in range(ends)]),
            ],
            axis=dim,
        )
    return cells


def precondition(field, precond):
    first, second, third = (field[:, 0], field[:, 1], field[:, 2])
    row_one = precond[:, 0] * first + precond[:, 3] * second + precond[:, 4] * third
    row_two = precond[:, 3] * first + precond[:, 1] * second + precond[:, 5] * third
    row_three = precond[:, 4] * first + precond[:, 5] * second + precond[:, 2] * third
    return jnp.stack([row_one, row_two, row_three], axis=1)


def exchange(rows, partial):
    shards = rows.shape[0]
    if partial is not None:
        extra = jnp.broadcast_to(partial.astype(jnp.float32), (shards, SIDE))
        rows = jnp.concatenate([rows, extra], axis=1)
    got = lax.all_to_all(rows, ("tod", "map"), split_axis=0, concat_axis=0, tiled=True)
    if partial is None:
        return got, None
    width = got.shape[1] - SIDE
    return got[:, :width], jnp.sum(got[:, width])


def read_kernel(slot_ref, maps_ref, offs_ref, cos_ref, sin_ref, out_ref):
    group = 8
    lanes = 128
    groups = offs_ref.shape[0] // group
    tile = offs_ref.shape[1]
    def body(g, carry):
        base = pl.multiple_of(g * group, group)
        rows = jnp.concatenate(
            [maps_ref[pl.ds(slot_ref[base + i], 1), :] for i in range(group)], axis=0
        )
        for j in range(tile // lanes):
            idx = offs_ref[pl.ds(base, group), pl.ds(j * lanes, lanes)]
            low = idx % lanes
            upper = idx >= lanes
            picked = []
            for s in range(3):
                first = rows[:, s * tile : s * tile + lanes]
                second = rows[:, s * tile + lanes : (s + 1) * tile]
                a = jnp.take_along_axis(first, low, axis=1, mode="promise_in_bounds")
                b = jnp.take_along_axis(second, low, axis=1, mode="promise_in_bounds")
                picked.append(jnp.where(upper, b, a))
            c = cos_ref[pl.ds(base, group), pl.ds(j * lanes, lanes)]
            sn = sin_ref[pl.ds(base, group), pl.ds(j * lanes, lanes)]
            out_ref[pl.ds(base, group), pl.ds(j * lanes, lanes)] = picked[0] + c * picked[1] + sn * picked[2]
        return carry
    lax.fori_loop(0, groups, body, 0)

def read(slots, maps, offs, cos, sin):
    nb, tile = offs.shape
    return pl.pallas_call(
        read_kernel,
        out_shape=jax.ShapeDtypeStruct((nb, tile), jnp.float32),
        grid_spec=pltpu.PrefetchScalarGridSpec(
            num_scalar_prefetch=1,
            grid=(1,),
            in_specs=[pl.BlockSpec(memory_space=pltpu.VMEM)] * 4,
            out_specs=pl.BlockSpec(memory_space=pltpu.VMEM),
        ),
    )(slots, maps, offs, cos, sin)


def local(tod, det_angle, angle_index, offsets, block_slot, hit_tiles, noise_filter, precond):
    shards = lax.axis_size(("tod", "map"))
    hits = hit_tiles[0]
    slot_count = hits.shape[1]
    owner_lists = lax.all_to_all(hits, ("tod", "map"), split_axis=0, concat_axis=0, tiled=True)
    tiles_dev = precond.shape[0]
    tile_pix = precond.shape[2]
    det_count, samp_count = tod.shape
    blocks_per_det = block_slot.shape[1]
    block_len = samp_count // blocks_per_det
    block_total = det_count * blocks_per_det
    hit_total = shards * slot_count
    split = 16
    while split * split < tile_pix:
        split *= 2
    low_count = tile_pix // split
    highest = lax.Precision.HIGH
    psi = det_angle[:, None] + jnp.pi * angle_index.astype(jnp.float32) / ANGLES
    stokes = jnp.stack([jnp.ones_like(psi), jnp.cos(2.0 * psi), jnp.sin(2.0 * psi)], axis=1)
    stokes_b = (
        stokes.reshape(det_count, 3, blocks_per_det, block_len)
        .transpose(0, 2, 1, 3)
        .reshape(block_total, 3, block_len)
    )
    cos_b = stokes[:, 1].reshape(block_total, block_len)
    sin_b = stokes[:, 2].reshape(block_total, block_len)
    placement = (
        owner_lists.reshape(-1)[:, None] == jnp.arange(tiles_dev, dtype=jnp.int32)[None, :]
    ).astype(jnp.float32)
    owner_flat = owner_lists.reshape(-1)
    owner_index = jnp.clip(owner_flat, 0, tiles_dev - 1)
    offs_b = offsets.reshape(block_total, block_len)
    high_hot = (
        (offs_b // low_count)[:, None, :] == jnp.arange(split, dtype=jnp.int32)[None, :, None]
    ).astype(jnp.float32)
    low_hot = (
        (offs_b % low_count)[:, None, :] == jnp.arange(low_count, dtype=jnp.int32)[None, :, None]
    ).astype(jnp.float32)

    band = noise_filter.shape[1] - 1
    rows = jnp.arange(3 * band, dtype=jnp.int32)[:, None]
    cols = jnp.arange(band, dtype=jnp.int32)[None, :]
    lag = jnp.abs(rows - cols - band)
    lag_hot = (lag[:, :, None] == jnp.arange(band + 1, dtype=jnp.int32)[None, None, :]).astype(
        jnp.float32
    )
    toeplitz = jnp.einsum(
        "dk,rck->drc", noise_filter, lag_hot, precision=highest, preferred_element_type=jnp.float32
    )
    block_count = samp_count // band

    def weigh(stream):
        padded = extended(stream, (("tod", 1),), band).reshape(det_count, block_count + 2, band)
        stacked = jnp.concatenate(
            [padded[:, k : k + block_count] for k in range(3)], axis=2
        )
        out = jnp.einsum(
            "dbj,dji->dbi",
            stacked,
            toeplitz,
            precision=highest,
            preferred_element_type=jnp.float32,
        )
        return out.reshape(det_count, samp_count)

    def binning(stream, partial):
        values = stokes_b * stream.reshape(block_total, 1, block_len)
        spread = values[:, :, None, :] * high_hot[:, None, :, :]
        block_maps = jnp.einsum(
            "bsan,bcn->bsac",
            spread,
            low_hot,
            precision=highest,
            preferred_element_type=jnp.float32,
        ).reshape(block_total, 3 * tile_pix)
        touched = jnp.zeros((hit_total, 3 * tile_pix), jnp.float32).at[block_slot.reshape(-1)].add(
            block_maps
        )
        arrived, total = exchange(touched.reshape(shards, slot_count * 3 * tile_pix), partial)
        summed = lax.dot_general(
            placement,
            arrived.reshape(hit_total, 3 * tile_pix),
            (((0,), (0,)), ((), ())),
            precision=highest,
            preferred_element_type=jnp.float32,
        )
        return summed.reshape(tiles_dev, 3, tile_pix), total

    def projection(field, partial):
        outgoing = jnp.where(
            (owner_flat >= 0)[:, None],
            jnp.take(field.reshape(tiles_dev, 3 * tile_pix), owner_index, axis=0),
            0.0,
        )
        touched, total = exchange(outgoing.reshape(shards, slot_count * 3 * tile_pix), partial)
        stream = read(
            block_slot.reshape(-1), touched.reshape(hit_total, 3 * tile_pix), offs_b, cos_b, sin_b
        )
        return stream.reshape(det_count, samp_count), total

    rhs, _ = binning(weigh(tod), None)
    solution = jnp.zeros_like(rhs)
    residual = rhs
    zeta = precondition(residual, precond)
    direction = zeta
    stream_dir, norm_now = projection(zeta, jnp.sum(residual * zeta))
    for step in range(ITERS):
        weighed = weigh(stream_dir)
        image, curvature = binning(weighed, jnp.sum(stream_dir * weighed))
        alpha = norm_now / curvature
        solution = solution + alpha * direction
        residual = residual - alpha * image
        if step + 1 < ITERS:
            zeta = precondition(residual, precond)
            stream_zeta, norm_next = projection(zeta, jnp.sum(residual * zeta))
            beta = norm_next / norm_now
            direction = zeta + beta * direction
            stream_dir = stream_zeta + beta * stream_dir
            norm_now = norm_next
    return (solution, residual)


def solution(mesh):
    in_specs = (
        P("map", "tod"),
        P("map"),
        P("map", "tod"),
        P("map", "tod"),
        P("map", "tod"),
        P(("tod", "map"), None, None),
        P("map", None),
        P(("tod", "map"), None, None),
    )
    out_specs = (P(("tod", "map"), None, None), P(("tod", "map"), None, None))
    return jax.shard_map(local, mesh=mesh, in_specs=in_specs, out_specs=out_specs, check_vma=False)
```

```python
import jax
import jax.numpy as jnp
from jax import lax
from jax.experimental import pallas as pl
from jax.experimental.pallas import tpu as pltpu
from jax.sharding import PartitionSpec as P

ANGLES = 64
ITERS = 2
SIDE = 128


def extended(cells, sides, width):
    for axis, dim in sides:
        count = lax.axis_size(axis)
        ends = count - 1
        head = lax.slice_in_dim(cells, 0, width, axis=dim)
        tail = lax.slice_in_dim(cells, cells.shape[dim] - width, cells.shape[dim], axis=dim)
        cells = jnp.concatenate(
            [
                lax.ppermute(tail, axis, [(i, (i + 1) % count) for i in range(ends)]),
                cells,
                lax.ppermute(head, axis, [((i + 1) % count, i) for i in range(ends)]),
            ],
            axis=dim,
        )
    return cells


def precondition(field, precond):
    first, second, third = (field[:, 0], field[:, 1], field[:, 2])
    row_one = precond[:, 0] * first + precond[:, 3] * second + precond[:, 4] * third
    row_two = precond[:, 3] * first + precond[:, 1] * second + precond[:, 5] * third
    row_three = precond[:, 4] * first + precond[:, 5] * second + precond[:, 2] * third
    return jnp.stack([row_one, row_two, row_three], axis=1)


def exchange(rows, partial):
    shards = rows.shape[0]
    if partial is not None:
        extra = jnp.broadcast_to(partial.astype(jnp.float32), (shards, SIDE))
        rows = jnp.concatenate([rows, extra], axis=1)
    got = lax.all_to_all(rows, ("tod", "map"), split_axis=0, concat_axis=0, tiled=True)
    if partial is None:
        return got, None
    width = got.shape[1] - SIDE
    return got[:, :width], jnp.sum(got[:, width])


def read_kernel(slot_ref, maps_ref, offs_ref, cos_ref, sin_ref, out_ref):
    group = 8
    lanes = 128
    groups = offs_ref.shape[0] // group
    tile = offs_ref.shape[1]
    def body(g, carry):
        base = pl.multiple_of(g * group, group)
        rows = jnp.concatenate(
            [maps_ref[pl.ds(slot_ref[base + i], 1), :] for i in range(group)], axis=0
        )
        for j in range(tile // lanes):
            idx = offs_ref[pl.ds(base, group), pl.ds(j * lanes, lanes)]
            low = idx % lanes
            upper = idx >= lanes
            picked = []
            for s in range(3):
                first = rows[:, s * tile : s * tile + lanes]
                second = rows[:, s * tile + lanes : (s + 1) * tile]
                a = jnp.take_along_axis(first, low, axis=1, mode="promise_in_bounds")
                b = jnp.take_along_axis(second, low, axis=1, mode="promise_in_bounds")
                picked.append(jnp.where(upper, b, a))
            c = cos_ref[pl.ds(base, group), pl.ds(j * lanes, lanes)]
            sn = sin_ref[pl.ds(base, group), pl.ds(j * lanes, lanes)]
            out_ref[pl.ds(base, group), pl.ds(j * lanes, lanes)] = picked[0] + c * picked[1] + sn * picked[2]
        return carry
    lax.fori_loop(0, groups, body, 0)

def read(slots, maps, offs, cos, sin):
    nb, tile = offs.shape
    return pl.pallas_call(
        read_kernel,
        out_shape=jax.ShapeDtypeStruct((nb, tile), jnp.float32),
        grid_spec=pltpu.PrefetchScalarGridSpec(
            num_scalar_prefetch=1,
            grid=(1,),
            in_specs=[pl.BlockSpec(memory_space=pltpu.VMEM)] * 4,
            out_specs=pl.BlockSpec(memory_space=pltpu.VMEM),
        ),
    )(slots, maps, offs, cos, sin)


def bin_kernel(slot_ref, offs_ref, y_ref, cos_ref, sin_ref, out_ref):
    group = 8
    blocks, tile = y_ref.shape
    out_ref[...] = jnp.zeros(out_ref.shape, out_ref.dtype)
    pix = lax.broadcasted_iota(jnp.int32, (tile, tile), 0)

    def body(g, carry):
        base = pl.multiple_of(g * group, group)
        y = y_ref[pl.ds(base, group), :]
        parts = [y, cos_ref[pl.ds(base, group), :] * y, sin_ref[pl.ds(base, group), :] * y]
        for i in range(group):
            rows = jnp.concatenate([p[i : i + 1] for p in parts], axis=0)
            high = rows.astype(jnp.bfloat16)
            rest = rows - high.astype(jnp.float32)
            mid = rest.astype(jnp.bfloat16)
            low = (rest - mid.astype(jnp.float32)).astype(jnp.bfloat16)
            stack = jnp.concatenate(
                [high, mid, low, jnp.zeros((16 - 9, tile), jnp.bfloat16)], axis=0
            )
            row = offs_ref[pl.ds(base + i, 1), :]
            hot = (row == pix).astype(jnp.bfloat16)
            res = lax.dot_general(
                stack, hot, (((1,), (1,)), ((), ())), preferred_element_type=jnp.float32
            )
            total = res[0:3] + res[3:6] + res[6:9]
            h = slot_ref[base + i]
            for s in range(3):
                cur = out_ref[pl.ds(h, 1), pl.ds(s * tile, tile)]
                out_ref[pl.ds(h, 1), pl.ds(s * tile, tile)] = cur + total[s : s + 1]
        return carry

    lax.fori_loop(0, blocks // group, body, 0)


def bin_call(slots, offs_t, y, cos, sin, hit_total):
    blocks, tile = y.shape
    return pl.pallas_call(
        bin_kernel,
        out_shape=jax.ShapeDtypeStruct((hit_total, 3 * tile), jnp.float32),
        grid_spec=pltpu.PrefetchScalarGridSpec(
            num_scalar_prefetch=1,
            grid=(1,),
            in_specs=[pl.BlockSpec(memory_space=pltpu.VMEM)] * 4,
            out_specs=pl.BlockSpec(memory_space=pltpu.VMEM),
        ),
    )(slots, offs_t, y, cos, sin)


def local(tod, det_angle, angle_index, offsets, block_slot, hit_tiles, noise_filter, precond):
    shards = lax.axis_size(("tod", "map"))
    hits = hit_tiles[0]
    slot_count = hits.shape[1]
    owner_lists = lax.all_to_all(hits, ("tod", "map"), split_axis=0, concat_axis=0, tiled=True)
    tiles_dev = precond.shape[0]
    tile_pix = precond.shape[2]
    det_count, samp_count = tod.shape
    blocks_per_det = block_slot.shape[1]
    block_len = samp_count // blocks_per_det
    block_total = det_count * blocks_per_det
    hit_total = shards * slot_count
    highest = lax.Precision.HIGH
    psi = det_angle[:, None] + jnp.pi * angle_index.astype(jnp.float32) / ANGLES
    stokes = jnp.stack([jnp.ones_like(psi), jnp.cos(2.0 * psi), jnp.sin(2.0 * psi)], axis=1)
    cos_b = stokes[:, 1].reshape(block_total, block_len)
    sin_b = stokes[:, 2].reshape(block_total, block_len)
    placement = (
        owner_lists.reshape(-1)[:, None] == jnp.arange(tiles_dev, dtype=jnp.int32)[None, :]
    ).astype(jnp.float32)
    owner_flat = owner_lists.reshape(-1)
    owner_index = jnp.clip(owner_flat, 0, tiles_dev - 1)
    offs_b = offsets.reshape(block_total, block_len)

    band = noise_filter.shape[1] - 1
    rows = jnp.arange(3 * band, dtype=jnp.int32)[:, None]
    cols = jnp.arange(band, dtype=jnp.int32)[None, :]
    lag = jnp.abs(rows - cols - band)
    lag_hot = (lag[:, :, None] == jnp.arange(band + 1, dtype=jnp.int32)[None, None, :]).astype(
        jnp.float32
    )
    toeplitz = jnp.einsum(
        "dk,rck->drc", noise_filter, lag_hot, precision=highest, preferred_element_type=jnp.float32
    )
    block_count = samp_count // band

    def weigh(stream):
        padded = extended(stream, (("tod", 1),), band).reshape(det_count, block_count + 2, band)
        stacked = jnp.concatenate(
            [padded[:, k : k + block_count] for k in range(3)], axis=2
        )
        out = jnp.einsum(
            "dbj,dji->dbi",
            stacked,
            toeplitz,
            precision=highest,
            preferred_element_type=jnp.float32,
        )
        return out.reshape(det_count, samp_count)

    def binning(stream, partial):
        touched = bin_call(
            block_slot.reshape(-1),
            offs_b,
            stream.reshape(block_total, block_len),
            cos_b,
            sin_b,
            hit_total,
        )
        arrived, total = exchange(touched.reshape(shards, slot_count * 3 * tile_pix), partial)
        summed = lax.dot_general(
            placement,
            arrived.reshape(hit_total, 3 * tile_pix),
            (((0,), (0,)), ((), ())),
            precision=highest,
            preferred_element_type=jnp.float32,
        )
        return summed.reshape(tiles_dev, 3, tile_pix), total

    def projection(field, partial):
        outgoing = jnp.where(
            (owner_flat >= 0)[:, None],
            jnp.take(field.reshape(tiles_dev, 3 * tile_pix), owner_index, axis=0),
            0.0,
        )
        touched, total = exchange(outgoing.reshape(shards, slot_count * 3 * tile_pix), partial)
        stream = read(
            block_slot.reshape(-1), touched.reshape(hit_total, 3 * tile_pix), offs_b, cos_b, sin_b
        )
        return stream.reshape(det_count, samp_count), total

    rhs, _ = binning(weigh(tod), None)
    solution = jnp.zeros_like(rhs)
    residual = rhs
    zeta = precondition(residual, precond)
    direction = zeta
    stream_dir, norm_now = projection(zeta, jnp.sum(residual * zeta))
    for step in range(ITERS):
        weighed = weigh(stream_dir)
        image, curvature = binning(weighed, jnp.sum(stream_dir * weighed))
        alpha = norm_now / curvature
        solution = solution + alpha * direction
        residual = residual - alpha * image
        if step + 1 < ITERS:
            zeta = precondition(residual, precond)
            stream_zeta, norm_next = projection(zeta, jnp.sum(residual * zeta))
            beta = norm_next / norm_now
            direction = zeta + beta * direction
            stream_dir = stream_zeta + beta * stream_dir
            norm_now = norm_next
    return (solution, residual)


def solution(mesh):
    in_specs = (
        P("map", "tod"),
        P("map"),
        P("map", "tod"),
        P("map", "tod"),
        P("map", "tod"),
        P(("tod", "map"), None, None),
        P("map", None),
        P(("tod", "map"), None, None),
    )
    out_specs = (P(("tod", "map"), None, None), P(("tod", "map"), None, None))
    return jax.shard_map(local, mesh=mesh, in_specs=in_specs, out_specs=out_specs, check_vma=False)
```

```python
import jax
import jax.numpy as jnp
from jax import lax
from jax.experimental import pallas as pl
from jax.experimental.pallas import tpu as pltpu
from jax.sharding import PartitionSpec as P

ANGLES = 64
ITERS = 2
SIDE = 128


def extended(cells, sides, width):
    for axis, dim in sides:
        count = lax.axis_size(axis)
        ends = count - 1
        head = lax.slice_in_dim(cells, 0, width, axis=dim)
        tail = lax.slice_in_dim(cells, cells.shape[dim] - width, cells.shape[dim], axis=dim)
        cells = jnp.concatenate(
            [
                lax.ppermute(tail, axis, [(i, (i + 1) % count) for i in range(ends)]),
                cells,
                lax.ppermute(head, axis, [((i + 1) % count, i) for i in range(ends)]),
            ],
            axis=dim,
        )
    return cells


def precondition(field, precond):
    first, second, third = (field[:, 0], field[:, 1], field[:, 2])
    row_one = precond[:, 0] * first + precond[:, 3] * second + precond[:, 4] * third
    row_two = precond[:, 3] * first + precond[:, 1] * second + precond[:, 5] * third
    row_three = precond[:, 4] * first + precond[:, 5] * second + precond[:, 2] * third
    return jnp.stack([row_one, row_two, row_three], axis=1)


def exchange(rows, partial):
    shards = rows.shape[0]
    if partial is not None:
        extra = jnp.broadcast_to(partial.astype(jnp.float32), (shards, SIDE))
        rows = jnp.concatenate([rows, extra], axis=1)
    got = lax.all_to_all(rows, ("tod", "map"), split_axis=0, concat_axis=0, tiled=True)
    if partial is None:
        return got, None
    width = got.shape[1] - SIDE
    return got[:, :width], jnp.sum(got[:, width])


GROUP = 8


def bin_kernel(slot_ref, offs_ref, y_ref, cos_ref, sin_ref, out_ref):
    dets, samples = y_ref.shape
    blocks = slot_ref.shape[0] // dets
    tile = samples // blocks
    out_ref[...] = jnp.zeros(out_ref.shape, out_ref.dtype)
    pix = lax.broadcasted_iota(jnp.int32, (tile, tile), 0)

    for first in range(0, dets, GROUP):
        def body(blk, carry):
            start = pl.multiple_of(blk * tile, tile)
            cols = pl.ds(start, tile)
            y = y_ref[first : first + GROUP, cols]
            offs = offs_ref[first : first + GROUP, cols]
            parts = [y, cos_ref[first : first + GROUP, cols] * y, sin_ref[first : first + GROUP, cols] * y]
            values = jnp.concatenate(parts, axis=0)
            high = values.astype(jnp.bfloat16)
            rest = values - high.astype(jnp.float32)
            mid = rest.astype(jnp.bfloat16)
            low = (rest - mid.astype(jnp.float32)).astype(jnp.bfloat16)
            for i in range(GROUP):
                stack = jnp.concatenate(
                    [piece[s * GROUP + i : s * GROUP + i + 1] for piece in (high, mid, low) for s in range(3)]
                    + [jnp.zeros((16 - 9, tile), jnp.bfloat16)],
                    axis=0,
                )
                hot = (offs[i : i + 1] == pix).astype(jnp.bfloat16)
                res = lax.dot_general(
                    stack, hot, (((1,), (1,)), ((), ())), preferred_element_type=jnp.float32
                )
                total = res[0:3] + res[3:6] + res[6:9]
                h = slot_ref[(first + i) * blocks + blk]
                for s in range(3):
                    spot = (pl.ds(h, 1), pl.ds(s * tile, tile))
                    out_ref[spot] = out_ref[spot] + total[s : s + 1]
            return carry

        lax.fori_loop(0, blocks, body, 0)


def bin_call(slots, offs, y, cos, sin, hit_total, tile):
    return pl.pallas_call(
        bin_kernel,
        out_shape=jax.ShapeDtypeStruct((hit_total, 3 * tile), jnp.float32),
        grid_spec=pltpu.PrefetchScalarGridSpec(
            num_scalar_prefetch=1,
            grid=(1,),
            in_specs=[pl.BlockSpec(memory_space=pltpu.VMEM)] * 4,
            out_specs=pl.BlockSpec(memory_space=pltpu.VMEM),
        ),
    )(slots, offs, y, cos, sin)


def read_kernel(slot_ref, maps_ref, offs_ref, cos_ref, sin_ref, out_ref):
    lanes = 128
    dets, samples = offs_ref.shape
    blocks = slot_ref.shape[0] // dets
    tile = maps_ref.shape[1] // 3

    for first in range(0, dets, GROUP):
        def body(blk, carry):
            rows = jnp.concatenate(
                [maps_ref[pl.ds(slot_ref[(first + i) * blocks + blk], 1), :] for i in range(GROUP)],
                axis=0,
            )
            for j in range(tile // lanes):
                start = pl.multiple_of(blk * tile + j * lanes, lanes)
                cols = pl.ds(start, lanes)
                idx = offs_ref[first : first + GROUP, cols]
                low = idx % lanes
                upper = idx >= lanes
                picked = []
                for s in range(3):
                    a = jnp.take_along_axis(
                        rows[:, s * tile : s * tile + lanes], low, axis=1, mode="promise_in_bounds"
                    )
                    b = jnp.take_along_axis(
                        rows[:, s * tile + lanes : (s + 1) * tile], low, axis=1, mode="promise_in_bounds"
                    )
                    picked.append(jnp.where(upper, b, a))
                c = cos_ref[first : first + GROUP, cols]
                sn = sin_ref[first : first + GROUP, cols]
                out_ref[first : first + GROUP, cols] = picked[0] + c * picked[1] + sn * picked[2]
            return carry

        lax.fori_loop(0, blocks, body, 0)


def read_call(slots, maps, offs, cos, sin):
    return pl.pallas_call(
        read_kernel,
        out_shape=jax.ShapeDtypeStruct(offs.shape, jnp.float32),
        grid_spec=pltpu.PrefetchScalarGridSpec(
            num_scalar_prefetch=1,
            grid=(1,),
            in_specs=[pl.BlockSpec(memory_space=pltpu.VMEM)] * 4,
            out_specs=pl.BlockSpec(memory_space=pltpu.VMEM),
        ),
    )(slots, maps, offs, cos, sin)


def local(tod, det_angle, angle_index, offsets, block_slot, hit_tiles, noise_filter, precond):
    shards = lax.axis_size(("tod", "map"))
    hits = hit_tiles[0]
    slot_count = hits.shape[1]
    owner_lists = lax.all_to_all(hits, ("tod", "map"), split_axis=0, concat_axis=0, tiled=True)
    tiles_dev = precond.shape[0]
    tile_pix = precond.shape[2]
    det_count, samp_count = tod.shape
    blocks_per_det = block_slot.shape[1]
    block_len = samp_count // blocks_per_det
    block_total = det_count * blocks_per_det
    hit_total = shards * slot_count
    highest = lax.Precision.HIGH
    psi = det_angle[:, None] + jnp.pi * angle_index.astype(jnp.float32) / ANGLES
    cosine = jnp.cos(2.0 * psi)
    sine = jnp.sin(2.0 * psi)
    placement = (
        owner_lists.reshape(-1)[:, None] == jnp.arange(tiles_dev, dtype=jnp.int32)[None, :]
    ).astype(jnp.float32)
    owner_flat = owner_lists.reshape(-1)
    owner_index = jnp.clip(owner_flat, 0, tiles_dev - 1)

    band = noise_filter.shape[1] - 1
    rows = jnp.arange(3 * band, dtype=jnp.int32)[:, None]
    cols = jnp.arange(band, dtype=jnp.int32)[None, :]
    lag = jnp.abs(rows - cols - band)
    lag_hot = (lag[:, :, None] == jnp.arange(band + 1, dtype=jnp.int32)[None, None, :]).astype(
        jnp.float32
    )
    toeplitz = jnp.einsum(
        "dk,rck->drc", noise_filter, lag_hot, precision=highest, preferred_element_type=jnp.float32
    )
    block_count = samp_count // band

    def weigh(stream):
        padded = extended(stream, (("tod", 1),), band).reshape(det_count, block_count + 2, band)
        stacked = jnp.concatenate(
            [padded[:, k : k + block_count] for k in range(3)], axis=2
        )
        out = jnp.einsum(
            "dbj,dji->dbi",
            stacked,
            toeplitz,
            precision=highest,
            preferred_element_type=jnp.float32,
        )
        return out.reshape(det_count, samp_count)

    def binning(stream, partial):
        touched = bin_call(block_slot.reshape(-1), offsets, stream, cosine, sine, hit_total, tile_pix)
        arrived, total = exchange(touched.reshape(shards, slot_count * 3 * tile_pix), partial)
        summed = lax.dot_general(
            placement,
            arrived.reshape(hit_total, 3 * tile_pix),
            (((0,), (0,)), ((), ())),
            precision=highest,
            preferred_element_type=jnp.float32,
        )
        return summed.reshape(tiles_dev, 3, tile_pix), total

    def projection(field, partial):
        outgoing = jnp.where(
            (owner_flat >= 0)[:, None],
            jnp.take(field.reshape(tiles_dev, 3 * tile_pix), owner_index, axis=0),
            0.0,
        )
        touched, total = exchange(outgoing.reshape(shards, slot_count * 3 * tile_pix), partial)
        stream = read_call(
            block_slot.reshape(-1), touched.reshape(hit_total, 3 * tile_pix), offsets, cosine, sine
        )
        return stream.reshape(det_count, samp_count), total

    rhs, _ = binning(weigh(tod), None)
    solution = jnp.zeros_like(rhs)
    residual = rhs
    zeta = precondition(residual, precond)
    direction = zeta
    stream_dir, norm_now = projection(zeta, jnp.sum(residual * zeta))
    for step in range(ITERS):
        weighed = weigh(stream_dir)
        image, curvature = binning(weighed, jnp.sum(stream_dir * weighed))
        alpha = norm_now / curvature
        solution = solution + alpha * direction
        residual = residual - alpha * image
        if step + 1 < ITERS:
            zeta = precondition(residual, precond)
            stream_zeta, norm_next = projection(zeta, jnp.sum(residual * zeta))
            beta = norm_next / norm_now
            direction = zeta + beta * direction
            stream_dir = stream_zeta + beta * stream_dir
            norm_now = norm_next
    return (solution, residual)


def solution(mesh):
    in_specs = (
        P("map", "tod"),
        P("map"),
        P("map", "tod"),
        P("map", "tod"),
        P("map", "tod"),
        P(("tod", "map"), None, None),
        P("map", None),
        P(("tod", "map"), None, None),
    )
    out_specs = (P(("tod", "map"), None, None), P(("tod", "map"), None, None))
    return jax.shard_map(local, mesh=mesh, in_specs=in_specs, out_specs=out_specs, check_vma=False)
```

```python
import jax
import jax.numpy as jnp
from jax import lax
from jax.experimental import pallas as pl
from jax.experimental.pallas import tpu as pltpu
from jax.sharding import PartitionSpec as P

ANGLES = 64
ITERS = 2
SIDE = 128


def extended(cells, sides, width):
    for axis, dim in sides:
        count = lax.axis_size(axis)
        ends = count - 1
        head = lax.slice_in_dim(cells, 0, width, axis=dim)
        tail = lax.slice_in_dim(cells, cells.shape[dim] - width, cells.shape[dim], axis=dim)
        cells = jnp.concatenate(
            [
                lax.ppermute(tail, axis, [(i, (i + 1) % count) for i in range(ends)]),
                cells,
                lax.ppermute(head, axis, [((i + 1) % count, i) for i in range(ends)]),
            ],
            axis=dim,
        )
    return cells


def precondition(field, precond):
    first, second, third = (field[:, 0], field[:, 1], field[:, 2])
    row_one = precond[:, 0] * first + precond[:, 3] * second + precond[:, 4] * third
    row_two = precond[:, 3] * first + precond[:, 1] * second + precond[:, 5] * third
    row_three = precond[:, 4] * first + precond[:, 5] * second + precond[:, 2] * third
    return jnp.stack([row_one, row_two, row_three], axis=1)


def exchange(rows, partial):
    shards = rows.shape[0]
    if partial is not None:
        extra = jnp.broadcast_to(partial.astype(jnp.float32), (shards, SIDE))
        rows = jnp.concatenate([rows, extra], axis=1)
    got = lax.all_to_all(rows, ("tod", "map"), split_axis=0, concat_axis=0, tiled=True)
    if partial is None:
        return got, None
    width = got.shape[1] - SIDE
    return got[:, :width], jnp.sum(got[:, width])


GROUP = 8


def bin_kernel(slot_ref, offs_ref, y_ref, cos_ref, sin_ref, out_ref):
    dets, samples = y_ref.shape
    blocks = slot_ref.shape[0] // dets
    tile = samples // blocks
    out_ref[...] = jnp.zeros(out_ref.shape, out_ref.dtype)
    half = tile // 2
    pix = lax.broadcasted_iota(jnp.int32, (half, tile), 0)

    for first in range(0, dets, GROUP):
        def body(blk, carry):
            start = pl.multiple_of(blk * tile, tile)
            cols = pl.ds(start, tile)
            y = y_ref[first : first + GROUP, cols]
            offs = offs_ref[first : first + GROUP, cols]
            parts = [y, cos_ref[first : first + GROUP, cols] * y, sin_ref[first : first + GROUP, cols] * y]
            values = jnp.concatenate(parts, axis=0)
            high = values.astype(jnp.bfloat16)
            rest = values - high.astype(jnp.float32)
            mid = rest.astype(jnp.bfloat16)
            low = (rest - mid.astype(jnp.float32)).astype(jnp.bfloat16)
            zero = jnp.zeros((1, tile), jnp.bfloat16)
            for i in range(GROUP):
                upper = offs[i : i + 1] >= half
                pieces = [piece[s * GROUP + i : s * GROUP + i + 1] for piece in (high, mid, low) for s in range(3)]
                stack = jnp.concatenate(
                    [jnp.where(upper, zero, r) for r in pieces]
                    + [jnp.where(upper, r, zero) for r in pieces]
                    + [jnp.zeros((32 - 18, tile), jnp.bfloat16)],
                    axis=0,
                )
                hot = ((offs[i : i + 1] % half) == pix).astype(jnp.bfloat16)
                res = lax.dot_general(
                    stack, hot, (((1,), (1,)), ((), ())), preferred_element_type=jnp.float32
                )
                below = res[0:3] + res[3:6] + res[6:9]
                above = res[9:12] + res[12:15] + res[15:18]
                total = jnp.concatenate([below, above], axis=1)
                h = slot_ref[(first + i) * blocks + blk]
                for s in range(3):
                    spot = (pl.ds(h, 1), pl.ds(s * tile, tile))
                    out_ref[spot] = out_ref[spot] + total[s : s + 1]
            return carry

        lax.fori_loop(0, blocks, body, 0)


def bin_call(slots, offs, y, cos, sin, hit_total, tile):
    return pl.pallas_call(
        bin_kernel,
        out_shape=jax.ShapeDtypeStruct((hit_total, 3 * tile), jnp.float32),
        grid_spec=pltpu.PrefetchScalarGridSpec(
            num_scalar_prefetch=1,
            grid=(1,),
            in_specs=[pl.BlockSpec(memory_space=pltpu.VMEM)] * 4,
            out_specs=pl.BlockSpec(memory_space=pltpu.VMEM),
        ),
    )(slots, offs, y, cos, sin)


def read_kernel(slot_ref, maps_ref, offs_ref, cos_ref, sin_ref, out_ref):
    lanes = 128
    dets, samples = offs_ref.shape
    blocks = slot_ref.shape[0] // dets
    tile = maps_ref.shape[1] // 3

    for first in range(0, dets, GROUP):
        def body(blk, carry):
            rows = jnp.concatenate(
                [maps_ref[pl.ds(slot_ref[(first + i) * blocks + blk], 1), :] for i in range(GROUP)],
                axis=0,
            )
            for j in range(tile // lanes):
                start = pl.multiple_of(blk * tile + j * lanes, lanes)
                cols = pl.ds(start, lanes)
                idx = offs_ref[first : first + GROUP, cols]
                low = idx % lanes
                upper = idx >= lanes
                picked = []
                for s in range(3):
                    a = jnp.take_along_axis(
                        rows[:, s * tile : s * tile + lanes], low, axis=1, mode="promise_in_bounds"
                    )
                    b = jnp.take_along_axis(
                        rows[:, s * tile + lanes : (s + 1) * tile], low, axis=1, mode="promise_in_bounds"
                    )
                    picked.append(jnp.where(upper, b, a))
                c = cos_ref[first : first + GROUP, cols]
                sn = sin_ref[first : first + GROUP, cols]
                out_ref[first : first + GROUP, cols] = picked[0] + c * picked[1] + sn * picked[2]
            return carry

        lax.fori_loop(0, blocks, body, 0)


def read_call(slots, maps, offs, cos, sin):
    return pl.pallas_call(
        read_kernel,
        out_shape=jax.ShapeDtypeStruct(offs.shape, jnp.float32),
        grid_spec=pltpu.PrefetchScalarGridSpec(
            num_scalar_prefetch=1,
            grid=(1,),
            in_specs=[pl.BlockSpec(memory_space=pltpu.VMEM)] * 4,
            out_specs=pl.BlockSpec(memory_space=pltpu.VMEM),
        ),
    )(slots, maps, offs, cos, sin)


def local(tod, det_angle, angle_index, offsets, block_slot, hit_tiles, noise_filter, precond):
    shards = lax.axis_size(("tod", "map"))
    hits = hit_tiles[0]
    slot_count = hits.shape[1]
    owner_lists = lax.all_to_all(hits, ("tod", "map"), split_axis=0, concat_axis=0, tiled=True)
    tiles_dev = precond.shape[0]
    tile_pix = precond.shape[2]
    det_count, samp_count = tod.shape
    blocks_per_det = block_slot.shape[1]
    block_len = samp_count // blocks_per_det
    block_total = det_count * blocks_per_det
    hit_total = shards * slot_count
    highest = lax.Precision.HIGH
    psi = det_angle[:, None] + jnp.pi * angle_index.astype(jnp.float32) / ANGLES
    cosine = jnp.cos(2.0 * psi)
    sine = jnp.sin(2.0 * psi)
    placement = (
        owner_lists.reshape(-1)[:, None] == jnp.arange(tiles_dev, dtype=jnp.int32)[None, :]
    ).astype(jnp.float32)
    owner_flat = owner_lists.reshape(-1)
    owner_index = jnp.clip(owner_flat, 0, tiles_dev - 1)

    band = noise_filter.shape[1] - 1
    rows = jnp.arange(3 * band, dtype=jnp.int32)[:, None]
    cols = jnp.arange(band, dtype=jnp.int32)[None, :]
    lag = jnp.abs(rows - cols - band)
    lag_hot = (lag[:, :, None] == jnp.arange(band + 1, dtype=jnp.int32)[None, None, :]).astype(
        jnp.float32
    )
    toeplitz = jnp.einsum(
        "dk,rck->drc", noise_filter, lag_hot, precision=highest, preferred_element_type=jnp.float32
    )
    block_count = samp_count // band

    def weigh(stream):
        padded = extended(stream, (("tod", 1),), band).reshape(det_count, block_count + 2, band)
        stacked = jnp.concatenate(
            [padded[:, k : k + block_count] for k in range(3)], axis=2
        )
        out = jnp.einsum(
            "dbj,dji->dbi",
            stacked,
            toeplitz,
            precision=highest,
            preferred_element_type=jnp.float32,
        )
        return out.reshape(det_count, samp_count)

    def binning(stream, partial):
        touched = bin_call(block_slot.reshape(-1), offsets, stream, cosine, sine, hit_total, tile_pix)
        arrived, total = exchange(touched.reshape(shards, slot_count * 3 * tile_pix), partial)
        summed = lax.dot_general(
            placement,
            arrived.reshape(hit_total, 3 * tile_pix),
            (((0,), (0,)), ((), ())),
            precision=highest,
            preferred_element_type=jnp.float32,
        )
        return summed.reshape(tiles_dev, 3, tile_pix), total

    def projection(field, partial):
        outgoing = jnp.where(
            (owner_flat >= 0)[:, None],
            jnp.take(field.reshape(tiles_dev, 3 * tile_pix), owner_index, axis=0),
            0.0,
        )
        touched, total = exchange(outgoing.reshape(shards, slot_count * 3 * tile_pix), partial)
        stream = read_call(
            block_slot.reshape(-1), touched.reshape(hit_total, 3 * tile_pix), offsets, cosine, sine
        )
        return stream.reshape(det_count, samp_count), total

    rhs, _ = binning(weigh(tod), None)
    solution = jnp.zeros_like(rhs)
    residual = rhs
    zeta = precondition(residual, precond)
    direction = zeta
    stream_dir, norm_now = projection(zeta, jnp.sum(residual * zeta))
    for step in range(ITERS):
        weighed = weigh(stream_dir)
        image, curvature = binning(weighed, jnp.sum(stream_dir * weighed))
        alpha = norm_now / curvature
        solution = solution + alpha * direction
        residual = residual - alpha * image
        if step + 1 < ITERS:
            zeta = precondition(residual, precond)
            stream_zeta, norm_next = projection(zeta, jnp.sum(residual * zeta))
            beta = norm_next / norm_now
            direction = zeta + beta * direction
            stream_dir = stream_zeta + beta * stream_dir
            norm_now = norm_next
    return (solution, residual)


def solution(mesh):
    in_specs = (
        P("map", "tod"),
        P("map"),
        P("map", "tod"),
        P("map", "tod"),
        P("map", "tod"),
        P(("tod", "map"), None, None),
        P("map", None),
        P(("tod", "map"), None, None),
    )
    out_specs = (P(("tod", "map"), None, None), P(("tod", "map"), None, None))
    return jax.shard_map(local, mesh=mesh, in_specs=in_specs, out_specs=out_specs, check_vma=False)
```

```python
import jax
import jax.numpy as jnp
from jax import lax
from jax.experimental import pallas as pl
from jax.experimental.pallas import tpu as pltpu
from jax.sharding import PartitionSpec as P

ANGLES = 64
ITERS = 2
SIDE = 128


def extended(cells, sides, width):
    for axis, dim in sides:
        count = lax.axis_size(axis)
        ends = count - 1
        head = lax.slice_in_dim(cells, 0, width, axis=dim)
        tail = lax.slice_in_dim(cells, cells.shape[dim] - width, cells.shape[dim], axis=dim)
        cells = jnp.concatenate(
            [
                lax.ppermute(tail, axis, [(i, (i + 1) % count) for i in range(ends)]),
                cells,
                lax.ppermute(head, axis, [((i + 1) % count, i) for i in range(ends)]),
            ],
            axis=dim,
        )
    return cells


def precondition(field, precond):
    first, second, third = (field[:, 0], field[:, 1], field[:, 2])
    row_one = precond[:, 0] * first + precond[:, 3] * second + precond[:, 4] * third
    row_two = precond[:, 3] * first + precond[:, 1] * second + precond[:, 5] * third
    row_three = precond[:, 4] * first + precond[:, 5] * second + precond[:, 2] * third
    return jnp.stack([row_one, row_two, row_three], axis=1)


def exchange(rows, partial, lists=None):
    shards = rows.shape[0]
    lane = jnp.arange(SIDE, dtype=jnp.int32)[None, :]
    extra = jnp.zeros((shards, SIDE), jnp.float32)
    if partial is not None:
        extra = jnp.where(lane == 0, partial.astype(jnp.float32), extra)
    if lists is not None:
        for k in range(lists.shape[1]):
            extra = jnp.where(lane == 1 + k, lists[:, k : k + 1].astype(jnp.float32), extra)
    rows = jnp.concatenate([rows, extra], axis=1)
    got = lax.all_to_all(rows, ("tod", "map"), split_axis=0, concat_axis=0, tiled=True)
    width = got.shape[1] - SIDE
    total = jnp.sum(got[:, width])
    if lists is None:
        return got[:, :width], total
    arrived_lists = jnp.round(got[:, width + 1 : width + 1 + lists.shape[1]]).astype(jnp.int32)
    return got[:, :width], total, arrived_lists


GROUP = 8


def bin_kernel(slot_ref, offs_ref, y_ref, cos_ref, sin_ref, out_ref):
    dets, samples = y_ref.shape
    blocks = slot_ref.shape[0] // dets
    tile = samples // blocks
    out_ref[...] = jnp.zeros(out_ref.shape, out_ref.dtype)
    half = tile // 2
    pix = lax.broadcasted_iota(jnp.int32, (half, tile), 0)

    for first in range(0, dets, GROUP):
        def body(blk, carry):
            start = pl.multiple_of(blk * tile, tile)
            cols = pl.ds(start, tile)
            y = y_ref[first : first + GROUP, cols]
            offs = offs_ref[first : first + GROUP, cols]
            parts = [y, cos_ref[first : first + GROUP, cols] * y, sin_ref[first : first + GROUP, cols] * y]
            values = jnp.concatenate(parts, axis=0)
            high = values.astype(jnp.bfloat16)
            rest = values - high.astype(jnp.float32)
            mid = rest.astype(jnp.bfloat16)
            low = (rest - mid.astype(jnp.float32)).astype(jnp.bfloat16)
            zero = jnp.zeros((1, tile), jnp.bfloat16)
            for i in range(GROUP):
                upper = offs[i : i + 1] >= half
                pieces = [piece[s * GROUP + i : s * GROUP + i + 1] for piece in (high, mid, low) for s in range(3)]
                stack = jnp.concatenate(
                    [jnp.where(upper, zero, r) for r in pieces]
                    + [jnp.where(upper, r, zero) for r in pieces]
                    + [jnp.zeros((32 - 18, tile), jnp.bfloat16)],
                    axis=0,
                )
                hot = ((offs[i : i + 1] % half) == pix).astype(jnp.bfloat16)
                res = lax.dot_general(
                    stack, hot, (((1,), (1,)), ((), ())), preferred_element_type=jnp.float32
                )
                below = res[0:3] + res[3:6] + res[6:9]
                above = res[9:12] + res[12:15] + res[15:18]
                total = jnp.concatenate([below, above], axis=1)
                h = slot_ref[(first + i) * blocks + blk]
                for s in range(3):
                    spot = (pl.ds(h, 1), pl.ds(s * tile, tile))
                    out_ref[spot] = out_ref[spot] + total[s : s + 1]
            return carry

        lax.fori_loop(0, blocks, body, 0)


def bin_call(slots, offs, y, cos, sin, hit_total, tile):
    return pl.pallas_call(
        bin_kernel,
        out_shape=jax.ShapeDtypeStruct((hit_total, 3 * tile), jnp.float32),
        grid_spec=pltpu.PrefetchScalarGridSpec(
            num_scalar_prefetch=1,
            grid=(1,),
            in_specs=[pl.BlockSpec(memory_space=pltpu.VMEM)] * 4,
            out_specs=pl.BlockSpec(memory_space=pltpu.VMEM),
        ),
    )(slots, offs, y, cos, sin)


def read_kernel(slot_ref, maps_ref, offs_ref, cos_ref, sin_ref, out_ref):
    lanes = 128
    dets, samples = offs_ref.shape
    blocks = slot_ref.shape[0] // dets
    tile = maps_ref.shape[1] // 3

    for first in range(0, dets, GROUP):
        def body(blk, carry):
            rows = jnp.concatenate(
                [maps_ref[pl.ds(slot_ref[(first + i) * blocks + blk], 1), :] for i in range(GROUP)],
                axis=0,
            )
            for j in range(tile // lanes):
                start = pl.multiple_of(blk * tile + j * lanes, lanes)
                cols = pl.ds(start, lanes)
                idx = offs_ref[first : first + GROUP, cols]
                low = idx % lanes
                upper = idx >= lanes
                picked = []
                for s in range(3):
                    a = jnp.take_along_axis(
                        rows[:, s * tile : s * tile + lanes], low, axis=1, mode="promise_in_bounds"
                    )
                    b = jnp.take_along_axis(
                        rows[:, s * tile + lanes : (s + 1) * tile], low, axis=1, mode="promise_in_bounds"
                    )
                    picked.append(jnp.where(upper, b, a))
                c = cos_ref[first : first + GROUP, cols]
                sn = sin_ref[first : first + GROUP, cols]
                out_ref[first : first + GROUP, cols] = picked[0] + c * picked[1] + sn * picked[2]
            return carry

        lax.fori_loop(0, blocks, body, 0)


def read_call(slots, maps, offs, cos, sin):
    return pl.pallas_call(
        read_kernel,
        out_shape=jax.ShapeDtypeStruct(offs.shape, jnp.float32),
        grid_spec=pltpu.PrefetchScalarGridSpec(
            num_scalar_prefetch=1,
            grid=(1,),
            in_specs=[pl.BlockSpec(memory_space=pltpu.VMEM)] * 4,
            out_specs=pl.BlockSpec(memory_space=pltpu.VMEM),
        ),
    )(slots, maps, offs, cos, sin)


def local(tod, det_angle, angle_index, offsets, block_slot, hit_tiles, noise_filter, precond):
    shards = lax.axis_size(("tod", "map"))
    hits = hit_tiles[0]
    slot_count = hits.shape[1]
    tiles_dev = precond.shape[0]
    tile_pix = precond.shape[2]
    det_count, samp_count = tod.shape
    blocks_per_det = block_slot.shape[1]
    block_len = samp_count // blocks_per_det
    block_total = det_count * blocks_per_det
    hit_total = shards * slot_count
    highest = lax.Precision.HIGH
    psi = det_angle[:, None] + jnp.pi * angle_index.astype(jnp.float32) / ANGLES
    cosine = jnp.cos(2.0 * psi)
    sine = jnp.sin(2.0 * psi)

    band = noise_filter.shape[1] - 1
    rows = jnp.arange(3 * band, dtype=jnp.int32)[:, None]
    cols = jnp.arange(band, dtype=jnp.int32)[None, :]
    lag = jnp.abs(rows - cols - band)
    lag_hot = (lag[:, :, None] == jnp.arange(band + 1, dtype=jnp.int32)[None, None, :]).astype(
        jnp.float32
    )
    toeplitz = jnp.einsum(
        "dk,rck->drc", noise_filter, lag_hot, precision=highest, preferred_element_type=jnp.float32
    )
    block_count = samp_count // band

    def weigh(stream):
        padded = extended(stream, (("tod", 1),), band).reshape(det_count, block_count + 2, band)
        stacked = jnp.concatenate(
            [padded[:, k : k + block_count] for k in range(3)], axis=2
        )
        out = jnp.einsum(
            "dbj,dji->dbi",
            stacked,
            toeplitz,
            precision=highest,
            preferred_element_type=jnp.float32,
        )
        return out.reshape(det_count, samp_count)

    def owner_sum(arrived, owner_flat, owner_index):
        kept = jnp.where((owner_flat >= 0)[:, None], arrived.reshape(hit_total, 3 * tile_pix), 0.0)
        summed = jnp.zeros((tiles_dev, 3 * tile_pix), jnp.float32).at[owner_index].add(kept)
        return summed.reshape(tiles_dev, 3, tile_pix)

    def binning(stream, partial):
        touched = bin_call(block_slot.reshape(-1), offsets, stream, cosine, sine, hit_total, tile_pix)
        arrived, total = exchange(touched.reshape(shards, slot_count * 3 * tile_pix), partial)
        return owner_sum(arrived, owner_flat, owner_index), total

    def projection(field, partial):
        outgoing = jnp.where(
            (owner_flat >= 0)[:, None],
            jnp.take(field.reshape(tiles_dev, 3 * tile_pix), owner_index, axis=0),
            0.0,
        )
        touched, total = exchange(outgoing.reshape(shards, slot_count * 3 * tile_pix), partial)
        stream = read_call(
            block_slot.reshape(-1), touched.reshape(hit_total, 3 * tile_pix), offsets, cosine, sine
        )
        return stream.reshape(det_count, samp_count), total

    touched = bin_call(block_slot.reshape(-1), offsets, weigh(tod), cosine, sine, hit_total, tile_pix)
    arrived, _, owner_lists = exchange(
        touched.reshape(shards, slot_count * 3 * tile_pix), None, hits
    )
    owner_flat = owner_lists.reshape(-1)
    owner_index = jnp.clip(owner_flat, 0, tiles_dev - 1)
    rhs = owner_sum(arrived, owner_flat, owner_index)
    solution = jnp.zeros_like(rhs)
    residual = rhs
    zeta = precondition(residual, precond)
    direction = zeta
    stream_dir, norm_now = projection(zeta, jnp.sum(residual * zeta))
    for step in range(ITERS):
        weighed = weigh(stream_dir)
        image, curvature = binning(weighed, jnp.sum(stream_dir * weighed))
        alpha = norm_now / curvature
        solution = solution + alpha * direction
        residual = residual - alpha * image
        if step + 1 < ITERS:
            zeta = precondition(residual, precond)
            stream_zeta, norm_next = projection(zeta, jnp.sum(residual * zeta))
            beta = norm_next / norm_now
            direction = zeta + beta * direction
            stream_dir = stream_zeta + beta * stream_dir
            norm_now = norm_next
    return (solution, residual)


def solution(mesh):
    in_specs = (
        P("map", "tod"),
        P("map"),
        P("map", "tod"),
        P("map", "tod"),
        P("map", "tod"),
        P(("tod", "map"), None, None),
        P("map", None),
        P(("tod", "map"), None, None),
    )
    out_specs = (P(("tod", "map"), None, None), P(("tod", "map"), None, None))
    return jax.shard_map(local, mesh=mesh, in_specs=in_specs, out_specs=out_specs, check_vma=False)
```

```python
import jax
import jax.numpy as jnp
from jax import lax
from jax.experimental import pallas as pl
from jax.experimental.pallas import tpu as pltpu
from jax.sharding import PartitionSpec as P

ANGLES = 64
ITERS = 2
SIDE = 128


def precondition(field, precond):
    first, second, third = (field[:, 0], field[:, 1], field[:, 2])
    row_one = precond[:, 0] * first + precond[:, 3] * second + precond[:, 4] * third
    row_two = precond[:, 3] * first + precond[:, 1] * second + precond[:, 5] * third
    row_three = precond[:, 4] * first + precond[:, 5] * second + precond[:, 2] * third
    return jnp.stack([row_one, row_two, row_three], axis=1)


def exchange(rows, partial, lists=None):
    shards = rows.shape[0]
    lane = jnp.arange(SIDE, dtype=jnp.int32)[None, :]
    extra = jnp.zeros((shards, SIDE), jnp.float32)
    if partial is not None:
        extra = jnp.where(lane == 0, partial.astype(jnp.float32), extra)
    if lists is not None:
        for k in range(lists.shape[1]):
            extra = jnp.where(lane == 1 + k, lists[:, k : k + 1].astype(jnp.float32), extra)
    rows = jnp.concatenate([rows, extra], axis=1)
    got = lax.all_to_all(rows, ("tod", "map"), split_axis=0, concat_axis=0, tiled=True)
    width = got.shape[1] - SIDE
    total = jnp.sum(got[:, width])
    if lists is None:
        return got[:, :width], total
    arrived_lists = jnp.round(got[:, width + 1 : width + 1 + lists.shape[1]]).astype(jnp.int32)
    return got[:, :width], total, arrived_lists


GROUP = 8


def bin_kernel(slot_ref, offs_ref, y_ref, cos_ref, sin_ref, out_ref):
    dets, samples = y_ref.shape
    blocks = slot_ref.shape[0] // dets
    tile = samples // blocks
    out_ref[...] = jnp.zeros(out_ref.shape, out_ref.dtype)
    half = tile // 2
    pix = lax.broadcasted_iota(jnp.int32, (half, tile), 0)

    for first in range(0, dets, GROUP):
        def body(blk, carry):
            start = pl.multiple_of(blk * tile, tile)
            cols = pl.ds(start, tile)
            y = y_ref[first : first + GROUP, cols]
            offs = offs_ref[first : first + GROUP, cols]
            parts = [y, cos_ref[first : first + GROUP, cols] * y, sin_ref[first : first + GROUP, cols] * y]
            values = jnp.concatenate(parts, axis=0)
            high = values.astype(jnp.bfloat16)
            rest = values - high.astype(jnp.float32)
            mid = rest.astype(jnp.bfloat16)
            low = (rest - mid.astype(jnp.float32)).astype(jnp.bfloat16)
            zero = jnp.zeros((1, tile), jnp.bfloat16)
            for i in range(GROUP):
                upper = offs[i : i + 1] >= half
                pieces = [piece[s * GROUP + i : s * GROUP + i + 1] for piece in (high, mid, low) for s in range(3)]
                stack = jnp.concatenate(
                    [jnp.where(upper, zero, r) for r in pieces]
                    + [jnp.where(upper, r, zero) for r in pieces]
                    + [jnp.zeros((32 - 18, tile), jnp.bfloat16)],
                    axis=0,
                )
                hot = ((offs[i : i + 1] % half) == pix).astype(jnp.bfloat16)
                res = lax.dot_general(
                    stack, hot, (((1,), (1,)), ((), ())), preferred_element_type=jnp.float32
                )
                below = res[0:3] + res[3:6] + res[6:9]
                above = res[9:12] + res[12:15] + res[15:18]
                total = jnp.concatenate([below, above], axis=1)
                h = slot_ref[(first + i) * blocks + blk]
                for s in range(3):
                    spot = (pl.ds(h, 1), pl.ds(s * tile, tile))
                    out_ref[spot] = out_ref[spot] + total[s : s + 1]
            return carry

        lax.fori_loop(0, blocks, body, 0)


def bin_call(slots, offs, y, cos, sin, hit_total, tile):
    return pl.pallas_call(
        bin_kernel,
        out_shape=jax.ShapeDtypeStruct((hit_total, 3 * tile), jnp.float32),
        grid_spec=pltpu.PrefetchScalarGridSpec(
            num_scalar_prefetch=1,
            grid=(1,),
            in_specs=[pl.BlockSpec(memory_space=pltpu.VMEM)] * 4,
            out_specs=pl.BlockSpec(memory_space=pltpu.VMEM),
        ),
    )(slots, offs, y, cos, sin)


def read_kernel(slot_ref, maps_ref, offs_ref, cos_ref, sin_ref, out_ref):
    lanes = 128
    dets, samples = offs_ref.shape
    blocks = slot_ref.shape[0] // dets
    tile = maps_ref.shape[1] // 3
    span = samples // blocks

    for first in range(0, dets, GROUP):
        def body(blk, carry):
            rows = jnp.concatenate(
                [maps_ref[pl.ds(slot_ref[(first + i) * blocks + blk], 1), :] for i in range(GROUP)],
                axis=0,
            )
            for j in range(span // lanes):
                start = pl.multiple_of(blk * span + j * lanes, lanes)
                cols = pl.ds(start, lanes)
                idx = offs_ref[first : first + GROUP, cols]
                low = idx % lanes
                upper = idx >= lanes
                picked = []
                for s in range(3):
                    a = jnp.take_along_axis(
                        rows[:, s * tile : s * tile + lanes], low, axis=1, mode="promise_in_bounds"
                    )
                    b = jnp.take_along_axis(
                        rows[:, s * tile + lanes : (s + 1) * tile], low, axis=1, mode="promise_in_bounds"
                    )
                    picked.append(jnp.where(upper, b, a))
                c = cos_ref[first : first + GROUP, cols]
                sn = sin_ref[first : first + GROUP, cols]
                out_ref[first : first + GROUP, cols] = picked[0] + c * picked[1] + sn * picked[2]
            return carry

        lax.fori_loop(0, blocks, body, 0)


def read_call(slots, maps, offs, cos, sin):
    return pl.pallas_call(
        read_kernel,
        out_shape=jax.ShapeDtypeStruct(offs.shape, jnp.float32),
        grid_spec=pltpu.PrefetchScalarGridSpec(
            num_scalar_prefetch=1,
            grid=(1,),
            in_specs=[pl.BlockSpec(memory_space=pltpu.VMEM)] * 4,
            out_specs=pl.BlockSpec(memory_space=pltpu.VMEM),
        ),
    )(slots, maps, offs, cos, sin)


def local(tod, det_angle, angle_index, offsets, block_slot, hit_tiles, noise_filter, precond):
    shards = lax.axis_size(("tod", "map"))
    hits = hit_tiles[0]
    slot_count = hits.shape[1]
    tiles_dev = precond.shape[0]
    tile_pix = precond.shape[2]
    det_count, samp_count = tod.shape
    blocks_per_det = block_slot.shape[1]
    block_len = samp_count // blocks_per_det
    block_total = det_count * blocks_per_det
    hit_total = shards * slot_count
    highest = lax.Precision.HIGH
    psi = det_angle[:, None] + jnp.pi * angle_index.astype(jnp.float32) / ANGLES
    cosine = jnp.cos(2.0 * psi)
    sine = jnp.sin(2.0 * psi)

    band = noise_filter.shape[1] - 1
    rows = jnp.arange(3 * band, dtype=jnp.int32)[:, None]
    cols = jnp.arange(band, dtype=jnp.int32)[None, :]
    lag = jnp.abs(rows - cols - band)
    lag_hot = (lag[:, :, None] == jnp.arange(band + 1, dtype=jnp.int32)[None, None, :]).astype(
        jnp.float32
    )
    toeplitz = jnp.einsum(
        "dk,rck->drc", noise_filter, lag_hot, precision=highest, preferred_element_type=jnp.float32
    )
    block_count = samp_count // band

    def halo(head, tail):
        count = lax.axis_size("tod")
        ends = count - 1
        from_left = lax.ppermute(tail, "tod", [(i, (i + 1) % count) for i in range(ends)])
        from_right = lax.ppermute(head, "tod", [((i + 1) % count, i) for i in range(ends)])
        return from_left, from_right

    def weigh(stream, sides):
        padded = jnp.concatenate([sides[0], stream, sides[1]], axis=1).reshape(
            det_count, block_count + 2, band
        )
        stacked = jnp.concatenate(
            [padded[:, k : k + block_count] for k in range(3)], axis=2
        )
        out = jnp.einsum(
            "dbj,dji->dbi",
            stacked,
            toeplitz,
            precision=highest,
            preferred_element_type=jnp.float32,
        )
        return out.reshape(det_count, samp_count)

    def owner_sum(arrived, owner_flat, owner_index):
        kept = jnp.where((owner_flat >= 0)[:, None], arrived.reshape(hit_total, 3 * tile_pix), 0.0)
        summed = jnp.zeros((tiles_dev, 3 * tile_pix), jnp.float32).at[owner_index].add(kept)
        return summed.reshape(tiles_dev, 3, tile_pix)

    def binning(stream, partial):
        touched = bin_call(block_slot.reshape(-1), offsets, stream, cosine, sine, hit_total, tile_pix)
        arrived, total = exchange(touched.reshape(shards, slot_count * 3 * tile_pix), partial)
        return owner_sum(arrived, owner_flat, owner_index), total

    def projection(field, partial):
        outgoing = jnp.where(
            (owner_flat >= 0)[:, None],
            jnp.take(field.reshape(tiles_dev, 3 * tile_pix), owner_index, axis=0),
            0.0,
        )
        touched, total = exchange(outgoing.reshape(shards, slot_count * 3 * tile_pix), partial)
        maps = touched.reshape(hit_total, 3 * tile_pix)
        edges = read_call(edge_slots, maps, edge_offs, edge_cos, edge_sin)
        sides = halo(edges[:, :band], edges[:, band:])
        stream = read_call(block_slot.reshape(-1), maps, offsets, cosine, sine)
        return stream, sides, total

    def edge_of(values):
        return jnp.concatenate([values[:, :band], values[:, samp_count - band :]], axis=1)

    edge_slots = jnp.stack([block_slot[:, 0], block_slot[:, blocks_per_det - 1]], axis=1).reshape(-1)
    edge_offs = edge_of(offsets)
    edge_cos = edge_of(cosine)
    edge_sin = edge_of(sine)
    tod_sides = halo(tod[:, :band], tod[:, samp_count - band :])
    touched = bin_call(
        block_slot.reshape(-1), offsets, weigh(tod, tod_sides), cosine, sine, hit_total, tile_pix
    )
    arrived, _, owner_lists = exchange(
        touched.reshape(shards, slot_count * 3 * tile_pix), None, hits
    )
    owner_flat = owner_lists.reshape(-1)
    owner_index = jnp.clip(owner_flat, 0, tiles_dev - 1)
    rhs = owner_sum(arrived, owner_flat, owner_index)
    solution = jnp.zeros_like(rhs)
    residual = rhs
    zeta = precondition(residual, precond)
    direction = zeta
    stream_dir, sides_dir, norm_now = projection(zeta, jnp.sum(residual * zeta))
    for step in range(ITERS):
        weighed = weigh(stream_dir, sides_dir)
        image, curvature = binning(weighed, jnp.sum(stream_dir * weighed))
        alpha = norm_now / curvature
        solution = solution + alpha * direction
        residual = residual - alpha * image
        if step + 1 < ITERS:
            zeta = precondition(residual, precond)
            stream_zeta, sides_zeta, norm_next = projection(zeta, jnp.sum(residual * zeta))
            beta = norm_next / norm_now
            direction = zeta + beta * direction
            stream_dir = stream_zeta + beta * stream_dir
            sides_dir = tuple(new + beta * old for new, old in zip(sides_zeta, sides_dir))
            norm_now = norm_next
    return (solution, residual)


def solution(mesh):
    in_specs = (
        P("map", "tod"),
        P("map"),
        P("map", "tod"),
        P("map", "tod"),
        P("map", "tod"),
        P(("tod", "map"), None, None),
        P("map", None),
        P(("tod", "map"), None, None),
    )
    out_specs = (P(("tod", "map"), None, None), P(("tod", "map"), None, None))
    return jax.shard_map(local, mesh=mesh, in_specs=in_specs, out_specs=out_specs, check_vma=False)
```

```python
import functools

import jax
import jax.numpy as jnp
from jax import lax
from jax.experimental import pallas as pl
from jax.experimental.pallas import tpu as pltpu
from jax.sharding import PartitionSpec as P

ANGLES = 64
ITERS = 2
SIDE = 128


def extended(cells, sides, width):
    for axis, dim in sides:
        count = lax.axis_size(axis)
        ends = count - 1
        head = lax.slice_in_dim(cells, 0, width, axis=dim)
        tail = lax.slice_in_dim(cells, cells.shape[dim] - width, cells.shape[dim], axis=dim)
        cells = jnp.concatenate(
            [
                lax.ppermute(tail, axis, [(i, (i + 1) % count) for i in range(ends)]),
                cells,
                lax.ppermute(head, axis, [((i + 1) % count, i) for i in range(ends)]),
            ],
            axis=dim,
        )
    return cells


def precondition(field, precond):
    first, second, third = (field[:, 0], field[:, 1], field[:, 2])
    row_one = precond[:, 0] * first + precond[:, 3] * second + precond[:, 4] * third
    row_two = precond[:, 3] * first + precond[:, 1] * second + precond[:, 5] * third
    row_three = precond[:, 4] * first + precond[:, 5] * second + precond[:, 2] * third
    return jnp.stack([row_one, row_two, row_three], axis=1)


def exchange(rows, partial, lists=None):
    shards = rows.shape[0]
    lane = jnp.arange(SIDE, dtype=jnp.int32)[None, :]
    extra = jnp.zeros((shards, SIDE), jnp.float32)
    if partial is not None:
        extra = jnp.where(lane == 0, partial.astype(jnp.float32), extra)
    if lists is not None:
        for k in range(lists.shape[1]):
            extra = jnp.where(lane == 1 + k, lists[:, k : k + 1].astype(jnp.float32), extra)
    rows = jnp.concatenate([rows, extra], axis=1)
    got = lax.all_to_all(rows, ("tod", "map"), split_axis=0, concat_axis=0, tiled=True)
    width = got.shape[1] - SIDE
    total = jnp.sum(got[:, width])
    if lists is None:
        return got, total
    arrived_lists = jnp.round(got[:, width + 1 : width + 1 + lists.shape[1]]).astype(jnp.int32)
    return got, total, arrived_lists


GROUP = 8


def bin_kernel(slot_ref, offs_ref, y_ref, cos_ref, sin_ref, out_ref, *, slots):
    dets, samples = y_ref.shape
    blocks = slot_ref.shape[0] // dets
    tile = samples // blocks
    out_ref[...] = jnp.zeros(out_ref.shape, out_ref.dtype)
    half = tile // 2
    pix = lax.broadcasted_iota(jnp.int32, (half, tile), 0)

    for first in range(0, dets, GROUP):
        def body(blk, carry):
            start = pl.multiple_of(blk * tile, tile)
            cols = pl.ds(start, tile)
            y = y_ref[first : first + GROUP, cols]
            offs = offs_ref[first : first + GROUP, cols]
            parts = [y, cos_ref[first : first + GROUP, cols] * y, sin_ref[first : first + GROUP, cols] * y]
            values = jnp.concatenate(parts, axis=0)
            high = values.astype(jnp.bfloat16)
            rest = values - high.astype(jnp.float32)
            mid = rest.astype(jnp.bfloat16)
            low = (rest - mid.astype(jnp.float32)).astype(jnp.bfloat16)
            zero = jnp.zeros((1, tile), jnp.bfloat16)
            for i in range(GROUP):
                upper = offs[i : i + 1] >= half
                pieces = [piece[s * GROUP + i : s * GROUP + i + 1] for piece in (high, mid, low) for s in range(3)]
                stack = jnp.concatenate(
                    [jnp.where(upper, zero, r) for r in pieces]
                    + [jnp.where(upper, r, zero) for r in pieces]
                    + [jnp.zeros((32 - 18, tile), jnp.bfloat16)],
                    axis=0,
                )
                hot = ((offs[i : i + 1] % half) == pix).astype(jnp.bfloat16)
                res = lax.dot_general(
                    stack, hot, (((1,), (1,)), ((), ())), preferred_element_type=jnp.float32
                )
                below = res[0:3] + res[3:6] + res[6:9]
                above = res[9:12] + res[12:15] + res[15:18]
                total = jnp.concatenate([below, above], axis=1)
                h = slot_ref[(first + i) * blocks + blk]
                row = h // slots
                lane = pl.multiple_of((h % slots) * (3 * tile), 128)
                for s in range(3):
                    spot = (pl.ds(row, 1), pl.ds(lane + s * tile, tile))
                    out_ref[spot] = out_ref[spot] + total[s : s + 1]
            return carry

        lax.fori_loop(0, blocks, body, 0)


def bin_call(slot_ids, offs, y, cos, sin, hit_total, tile, slots):
    return pl.pallas_call(
        functools.partial(bin_kernel, slots=slots),
        out_shape=jax.ShapeDtypeStruct((hit_total // slots, slots * 3 * tile), jnp.float32),
        grid_spec=pltpu.PrefetchScalarGridSpec(
            num_scalar_prefetch=1,
            grid=(1,),
            in_specs=[pl.BlockSpec(memory_space=pltpu.VMEM)] * 4,
            out_specs=pl.BlockSpec(memory_space=pltpu.VMEM),
        ),
    )(slot_ids, offs, y, cos, sin)


def read_kernel(slot_ref, maps_ref, offs_ref, cos_ref, sin_ref, out_ref, *, tile, slots):
    lanes = 128
    dets, samples = offs_ref.shape
    blocks = slot_ref.shape[0] // dets

    for first in range(0, dets, GROUP):
        def body(blk, carry):
            rows = jnp.concatenate(
                [
                    maps_ref[
                        pl.ds(slot_ref[(first + i) * blocks + blk] // slots, 1),
                        pl.ds(
                            pl.multiple_of((slot_ref[(first + i) * blocks + blk] % slots) * (3 * tile), 128),
                            3 * tile,
                        ),
                    ]
                    for i in range(GROUP)
                ],
                axis=0,
            )
            for j in range(tile // lanes):
                start = pl.multiple_of(blk * tile + j * lanes, lanes)
                cols = pl.ds(start, lanes)
                idx = offs_ref[first : first + GROUP, cols]
                low = idx % lanes
                upper = idx >= lanes
                picked = []
                for s in range(3):
                    a = jnp.take_along_axis(
                        rows[:, s * tile : s * tile + lanes], low, axis=1, mode="promise_in_bounds"
                    )
                    b = jnp.take_along_axis(
                        rows[:, s * tile + lanes : (s + 1) * tile], low, axis=1, mode="promise_in_bounds"
                    )
                    picked.append(jnp.where(upper, b, a))
                c = cos_ref[first : first + GROUP, cols]
                sn = sin_ref[first : first + GROUP, cols]
                out_ref[first : first + GROUP, cols] = picked[0] + c * picked[1] + sn * picked[2]
            return carry

        lax.fori_loop(0, blocks, body, 0)


def read_call(slot_ids, maps, offs, cos, sin, tile, slots):
    return pl.pallas_call(
        functools.partial(read_kernel, tile=tile, slots=slots),
        out_shape=jax.ShapeDtypeStruct(offs.shape, jnp.float32),
        grid_spec=pltpu.PrefetchScalarGridSpec(
            num_scalar_prefetch=1,
            grid=(1,),
            in_specs=[pl.BlockSpec(memory_space=pltpu.VMEM)] * 4,
            out_specs=pl.BlockSpec(memory_space=pltpu.VMEM),
        ),
    )(slot_ids, maps, offs, cos, sin)


def local(tod, det_angle, angle_index, offsets, block_slot, hit_tiles, noise_filter, precond):
    shards = lax.axis_size(("tod", "map"))
    hits = hit_tiles[0]
    slot_count = hits.shape[1]
    tiles_dev = precond.shape[0]
    tile_pix = precond.shape[2]
    det_count, samp_count = tod.shape
    blocks_per_det = block_slot.shape[1]
    block_len = samp_count // blocks_per_det
    block_total = det_count * blocks_per_det
    hit_total = shards * slot_count
    highest = lax.Precision.HIGH
    psi = det_angle[:, None] + jnp.pi * angle_index.astype(jnp.float32) / ANGLES
    cosine = jnp.cos(2.0 * psi)
    sine = jnp.sin(2.0 * psi)

    band = noise_filter.shape[1] - 1
    rows = jnp.arange(3 * band, dtype=jnp.int32)[:, None]
    cols = jnp.arange(band, dtype=jnp.int32)[None, :]
    lag = jnp.abs(rows - cols - band)
    lag_hot = (lag[:, :, None] == jnp.arange(band + 1, dtype=jnp.int32)[None, None, :]).astype(
        jnp.float32
    )
    toeplitz = jnp.einsum(
        "dk,rck->drc", noise_filter, lag_hot, precision=highest, preferred_element_type=jnp.float32
    )
    block_count = samp_count // band

    def weigh(stream):
        padded = extended(stream, (("tod", 1),), band).reshape(det_count, block_count + 2, band)
        stacked = jnp.concatenate(
            [padded[:, k : k + block_count] for k in range(3)], axis=2
        )
        out = jnp.einsum(
            "dbj,dji->dbi",
            stacked,
            toeplitz,
            precision=highest,
            preferred_element_type=jnp.float32,
        )
        return out.reshape(det_count, samp_count)

    def owner_sum(arrived, owner_lists):
        summed = jnp.zeros((tiles_dev, 3 * tile_pix), jnp.float32)
        for j in range(slot_count):
            lists = owner_lists[:, j]
            part = arrived[:, j * 3 * tile_pix : (j + 1) * 3 * tile_pix]
            kept = jnp.where((lists >= 0)[:, None], part, 0.0)
            summed = summed.at[jnp.clip(lists, 0, tiles_dev - 1)].add(kept)
        return summed.reshape(tiles_dev, 3, tile_pix)

    def binning(stream, partial):
        touched = bin_call(
            block_slot.reshape(-1), offsets, stream, cosine, sine, hit_total, tile_pix, slot_count
        )
        arrived, total = exchange(touched, partial)
        return owner_sum(arrived, owner_lists), total

    def projection(field, partial):
        outgoing = jnp.where(
            (owner_flat >= 0)[:, None],
            jnp.take(field.reshape(tiles_dev, 3 * tile_pix), owner_index, axis=0),
            0.0,
        )
        touched, total = exchange(outgoing.reshape(shards, slot_count * 3 * tile_pix), partial)
        stream = read_call(block_slot.reshape(-1), touched, offsets, cosine, sine, tile_pix, slot_count)
        return stream.reshape(det_count, samp_count), total

    touched = bin_call(
        block_slot.reshape(-1), offsets, weigh(tod), cosine, sine, hit_total, tile_pix, slot_count
    )
    arrived, _, owner_lists = exchange(touched, None, hits)
    owner_flat = owner_lists.reshape(-1)
    owner_index = jnp.clip(owner_flat, 0, tiles_dev - 1)
    rhs = owner_sum(arrived, owner_lists)
    solution = jnp.zeros_like(rhs)
    residual = rhs
    zeta = precondition(residual, precond)
    direction = zeta
    stream_dir, norm_now = projection(zeta, jnp.sum(residual * zeta))
    for step in range(ITERS):
        weighed = weigh(stream_dir)
        image, curvature = binning(weighed, jnp.sum(stream_dir * weighed))
        alpha = norm_now / curvature
        solution = solution + alpha * direction
        residual = residual - alpha * image
        if step + 1 < ITERS:
            zeta = precondition(residual, precond)
            stream_zeta, norm_next = projection(zeta, jnp.sum(residual * zeta))
            beta = norm_next / norm_now
            direction = zeta + beta * direction
            stream_dir = stream_zeta + beta * stream_dir
            norm_now = norm_next
    return (solution, residual)


def solution(mesh):
    in_specs = (
        P("map", "tod"),
        P("map"),
        P("map", "tod"),
        P("map", "tod"),
        P("map", "tod"),
        P(("tod", "map"), None, None),
        P("map", None),
        P(("tod", "map"), None, None),
    )
    out_specs = (P(("tod", "map"), None, None), P(("tod", "map"), None, None))
    return jax.shard_map(local, mesh=mesh, in_specs=in_specs, out_specs=out_specs, check_vma=False)
```

```python
import jax
import jax.numpy as jnp
from jax import lax
from jax.experimental import pallas as pl
from jax.experimental.pallas import tpu as pltpu
from jax.sharding import PartitionSpec as P

ANGLES = 64
ITERS = 2
SIDE = 128


def extended(cells, sides, width):
    for axis, dim in sides:
        count = lax.axis_size(axis)
        ends = count - 1
        head = lax.slice_in_dim(cells, 0, width, axis=dim)
        tail = lax.slice_in_dim(cells, cells.shape[dim] - width, cells.shape[dim], axis=dim)
        cells = jnp.concatenate(
            [
                lax.ppermute(tail, axis, [(i, (i + 1) % count) for i in range(ends)]),
                cells,
                lax.ppermute(head, axis, [((i + 1) % count, i) for i in range(ends)]),
            ],
            axis=dim,
        )
    return cells


def precondition(field, precond):
    tile = precond.shape[2]
    first, second, third = (field[:, 0:tile], field[:, tile : 2 * tile], field[:, 2 * tile :])
    row_one = precond[:, 0] * first + precond[:, 3] * second + precond[:, 4] * third
    row_two = precond[:, 3] * first + precond[:, 1] * second + precond[:, 5] * third
    row_three = precond[:, 4] * first + precond[:, 5] * second + precond[:, 2] * third
    return jnp.concatenate([row_one, row_two, row_three], axis=1)


def exchange(rows, partial, lists=None):
    shards = rows.shape[0]
    lane = jnp.arange(SIDE, dtype=jnp.int32)[None, :]
    extra = jnp.zeros((shards, SIDE), jnp.float32)
    if partial is not None:
        extra = jnp.where(lane == 0, partial.astype(jnp.float32), extra)
    if lists is not None:
        for k in range(lists.shape[1]):
            extra = jnp.where(lane == 1 + k, lists[:, k : k + 1].astype(jnp.float32), extra)
    rows = jnp.concatenate([rows, extra], axis=1)
    got = lax.all_to_all(rows, ("tod", "map"), split_axis=0, concat_axis=0, tiled=True)
    width = got.shape[1] - SIDE
    total = jnp.sum(got[:, width])
    if lists is None:
        return got[:, :width], total
    arrived_lists = jnp.round(got[:, width + 1 : width + 1 + lists.shape[1]]).astype(jnp.int32)
    return got[:, :width], total, arrived_lists


GROUP = 8


def bin_kernel(slot_ref, offs_ref, y_ref, cos_ref, sin_ref, out_ref):
    dets, samples = y_ref.shape
    blocks = slot_ref.shape[0] // dets
    tile = samples // blocks
    out_ref[...] = jnp.zeros(out_ref.shape, out_ref.dtype)
    half = tile // 2
    pix = lax.broadcasted_iota(jnp.int32, (half, tile), 0)

    for first in range(0, dets, GROUP):
        def body(blk, carry):
            start = pl.multiple_of(blk * tile, tile)
            cols = pl.ds(start, tile)
            y = y_ref[first : first + GROUP, cols]
            offs = offs_ref[first : first + GROUP, cols]
            parts = [y, cos_ref[first : first + GROUP, cols] * y, sin_ref[first : first + GROUP, cols] * y]
            values = jnp.concatenate(parts, axis=0)
            high = values.astype(jnp.bfloat16)
            rest = values - high.astype(jnp.float32)
            mid = rest.astype(jnp.bfloat16)
            low = (rest - mid.astype(jnp.float32)).astype(jnp.bfloat16)
            zero = jnp.zeros((1, tile), jnp.bfloat16)
            for i in range(GROUP):
                upper = offs[i : i + 1] >= half
                pieces = [piece[s * GROUP + i : s * GROUP + i + 1] for piece in (high, mid, low) for s in range(3)]
                stack = jnp.concatenate(
                    [jnp.where(upper, zero, r) for r in pieces]
                    + [jnp.where(upper, r, zero) for r in pieces]
                    + [jnp.zeros((32 - 18, tile), jnp.bfloat16)],
                    axis=0,
                )
                hot = ((offs[i : i + 1] % half) == pix).astype(jnp.bfloat16)
                res = lax.dot_general(
                    stack, hot, (((1,), (1,)), ((), ())), preferred_element_type=jnp.float32
                )
                below = res[0:3] + res[3:6] + res[6:9]
                above = res[9:12] + res[12:15] + res[15:18]
                total = jnp.concatenate([below, above], axis=1)
                h = slot_ref[(first + i) * blocks + blk]
                for s in range(3):
                    spot = (pl.ds(h, 1), pl.ds(s * tile, tile))
                    out_ref[spot] = out_ref[spot] + total[s : s + 1]
            return carry

        lax.fori_loop(0, blocks, body, 0)


def bin_call(slots, offs, y, cos, sin, hit_total, tile):
    return pl.pallas_call(
        bin_kernel,
        out_shape=jax.ShapeDtypeStruct((hit_total, 3 * tile), jnp.float32),
        grid_spec=pltpu.PrefetchScalarGridSpec(
            num_scalar_prefetch=1,
            grid=(1,),
            in_specs=[pl.BlockSpec(memory_space=pltpu.VMEM)] * 4,
            out_specs=pl.BlockSpec(memory_space=pltpu.VMEM),
        ),
    )(slots, offs, y, cos, sin)


def read_kernel(slot_ref, maps_ref, offs_ref, cos_ref, sin_ref, out_ref):
    lanes = 128
    dets, samples = offs_ref.shape
    blocks = slot_ref.shape[0] // dets
    tile = maps_ref.shape[1] // 3

    for first in range(0, dets, GROUP):
        def body(blk, carry):
            rows = jnp.concatenate(
                [maps_ref[pl.ds(slot_ref[(first + i) * blocks + blk], 1), :] for i in range(GROUP)],
                axis=0,
            )
            for j in range(tile // lanes):
                start = pl.multiple_of(blk * tile + j * lanes, lanes)
                cols = pl.ds(start, lanes)
                idx = offs_ref[first : first + GROUP, cols]
                low = idx % lanes
                upper = idx >= lanes
                picked = []
                for s in range(3):
                    a = jnp.take_along_axis(
                        rows[:, s * tile : s * tile + lanes], low, axis=1, mode="promise_in_bounds"
                    )
                    b = jnp.take_along_axis(
                        rows[:, s * tile + lanes : (s + 1) * tile], low, axis=1, mode="promise_in_bounds"
                    )
                    picked.append(jnp.where(upper, b, a))
                c = cos_ref[first : first + GROUP, cols]
                sn = sin_ref[first : first + GROUP, cols]
                out_ref[first : first + GROUP, cols] = picked[0] + c * picked[1] + sn * picked[2]
            return carry

        lax.fori_loop(0, blocks, body, 0)


def read_call(slots, maps, offs, cos, sin):
    return pl.pallas_call(
        read_kernel,
        out_shape=jax.ShapeDtypeStruct(offs.shape, jnp.float32),
        grid_spec=pltpu.PrefetchScalarGridSpec(
            num_scalar_prefetch=1,
            grid=(1,),
            in_specs=[pl.BlockSpec(memory_space=pltpu.VMEM)] * 4,
            out_specs=pl.BlockSpec(memory_space=pltpu.VMEM),
        ),
    )(slots, maps, offs, cos, sin)


def local(tod, det_angle, angle_index, offsets, block_slot, hit_tiles, noise_filter, precond):
    shards = lax.axis_size(("tod", "map"))
    hits = hit_tiles[0]
    slot_count = hits.shape[1]
    tiles_dev = precond.shape[0]
    tile_pix = precond.shape[2]
    det_count, samp_count = tod.shape
    blocks_per_det = block_slot.shape[1]
    block_len = samp_count // blocks_per_det
    block_total = det_count * blocks_per_det
    hit_total = shards * slot_count
    highest = lax.Precision.HIGH
    psi = det_angle[:, None] + jnp.pi * angle_index.astype(jnp.float32) / ANGLES
    cosine = jnp.cos(2.0 * psi)
    sine = jnp.sin(2.0 * psi)

    band = noise_filter.shape[1] - 1
    rows = jnp.arange(3 * band, dtype=jnp.int32)[:, None]
    cols = jnp.arange(band, dtype=jnp.int32)[None, :]
    lag = jnp.abs(rows - cols - band)
    lag_hot = (lag[:, :, None] == jnp.arange(band + 1, dtype=jnp.int32)[None, None, :]).astype(
        jnp.float32
    )
    toeplitz = jnp.einsum(
        "dk,rck->drc", noise_filter, lag_hot, precision=highest, preferred_element_type=jnp.float32
    )
    block_count = samp_count // band

    def weigh(stream):
        padded = extended(stream, (("tod", 1),), band).reshape(det_count, block_count + 2, band)
        stacked = jnp.concatenate(
            [padded[:, k : k + block_count] for k in range(3)], axis=2
        )
        out = jnp.einsum(
            "dbj,dji->dbi",
            stacked,
            toeplitz,
            precision=highest,
            preferred_element_type=jnp.float32,
        )
        return out.reshape(det_count, samp_count)

    def owner_sum(arrived, owner_flat, owner_index):
        kept = jnp.where((owner_flat >= 0)[:, None], arrived.reshape(hit_total, 3 * tile_pix), 0.0)
        summed = jnp.zeros((tiles_dev, 3 * tile_pix), jnp.float32).at[owner_index].add(kept)
        return summed

    def binning(stream, partial):
        touched = bin_call(block_slot.reshape(-1), offsets, stream, cosine, sine, hit_total, tile_pix)
        arrived, total = exchange(touched.reshape(shards, slot_count * 3 * tile_pix), partial)
        return owner_sum(arrived, owner_flat, owner_index), total

    def projection(field, partial):
        outgoing = jnp.where(
            (owner_flat >= 0)[:, None],
            jnp.take(field, owner_index, axis=0),
            0.0,
        )
        touched, total = exchange(outgoing.reshape(shards, slot_count * 3 * tile_pix), partial)
        stream = read_call(
            block_slot.reshape(-1), touched.reshape(hit_total, 3 * tile_pix), offsets, cosine, sine
        )
        return stream.reshape(det_count, samp_count), total

    touched = bin_call(block_slot.reshape(-1), offsets, weigh(tod), cosine, sine, hit_total, tile_pix)
    arrived, _, owner_lists = exchange(
        touched.reshape(shards, slot_count * 3 * tile_pix), None, hits
    )
    owner_flat = owner_lists.reshape(-1)
    owner_index = jnp.clip(owner_flat, 0, tiles_dev - 1)
    rhs = owner_sum(arrived, owner_flat, owner_index)
    solution = jnp.zeros_like(rhs)
    residual = rhs
    zeta = precondition(residual, precond)
    direction = zeta
    stream_dir, norm_now = projection(zeta, jnp.sum(residual * zeta))
    for step in range(ITERS):
        weighed = weigh(stream_dir)
        image, curvature = binning(weighed, jnp.sum(stream_dir * weighed))
        alpha = norm_now / curvature
        solution = solution + alpha * direction
        residual = residual - alpha * image
        if step + 1 < ITERS:
            zeta = precondition(residual, precond)
            stream_zeta, norm_next = projection(zeta, jnp.sum(residual * zeta))
            beta = norm_next / norm_now
            direction = zeta + beta * direction
            stream_dir = stream_zeta + beta * stream_dir
            norm_now = norm_next
    return (solution.reshape(tiles_dev, 3, tile_pix), residual.reshape(tiles_dev, 3, tile_pix))


def solution(mesh):
    in_specs = (
        P("map", "tod"),
        P("map"),
        P("map", "tod"),
        P("map", "tod"),
        P("map", "tod"),
        P(("tod", "map"), None, None),
        P("map", None),
        P(("tod", "map"), None, None),
    )
    out_specs = (P(("tod", "map"), None, None), P(("tod", "map"), None, None))
    return jax.shard_map(local, mesh=mesh, in_specs=in_specs, out_specs=out_specs, check_vma=False)
```

```python
import functools

import jax
import jax.numpy as jnp
from jax import lax
from jax.experimental import pallas as pl
from jax.experimental.pallas import tpu as pltpu
from jax.sharding import PartitionSpec as P

ANGLES = 64
ITERS = 2
SIDE = 128


def extended(cells, sides, width):
    for axis, dim in sides:
        count = lax.axis_size(axis)
        ends = count - 1
        head = lax.slice_in_dim(cells, 0, width, axis=dim)
        tail = lax.slice_in_dim(cells, cells.shape[dim] - width, cells.shape[dim], axis=dim)
        cells = jnp.concatenate(
            [
                lax.ppermute(tail, axis, [(i, (i + 1) % count) for i in range(ends)]),
                cells,
                lax.ppermute(head, axis, [((i + 1) % count, i) for i in range(ends)]),
            ],
            axis=dim,
        )
    return cells


def precondition(field, precond):
    tile = precond.shape[2]
    first, second, third = (field[:, 0:tile], field[:, tile : 2 * tile], field[:, 2 * tile :])
    row_one = precond[:, 0] * first + precond[:, 3] * second + precond[:, 4] * third
    row_two = precond[:, 3] * first + precond[:, 1] * second + precond[:, 5] * third
    row_three = precond[:, 4] * first + precond[:, 5] * second + precond[:, 2] * third
    return jnp.concatenate([row_one, row_two, row_three], axis=1)


def exchange(rows, partial, lists=None):
    shards = rows.shape[0]
    lane = jnp.arange(SIDE, dtype=jnp.int32)[None, :]
    extra = jnp.zeros((shards, SIDE), jnp.float32)
    if partial is not None:
        extra = jnp.where(lane == 0, partial.astype(jnp.float32), extra)
    if lists is not None:
        for k in range(lists.shape[1]):
            extra = jnp.where(lane == 1 + k, lists[:, k : k + 1].astype(jnp.float32), extra)
    rows = jnp.concatenate([rows, extra], axis=1)
    got = lax.all_to_all(rows, ("tod", "map"), split_axis=0, concat_axis=0, tiled=True)
    width = got.shape[1] - SIDE
    total = jnp.sum(got[:, width])
    if lists is None:
        return got[:, :width], total
    arrived_lists = jnp.round(got[:, width + 1 : width + 1 + lists.shape[1]]).astype(jnp.int32)
    return got[:, :width], total, arrived_lists


GROUP = 8


def bin_kernel(slot_ref, offs_ref, y_ref, cos_ref, sin_ref, out_ref, *, slots):
    dets, samples = y_ref.shape
    blocks = slot_ref.shape[0] // dets
    tile = samples // blocks
    out_ref[...] = jnp.zeros(out_ref.shape, out_ref.dtype)
    half = tile // 2
    pix = lax.broadcasted_iota(jnp.int32, (half, tile), 0)

    for first in range(0, dets, GROUP):
        def body(blk, carry):
            start = pl.multiple_of(blk * tile, tile)
            cols = pl.ds(start, tile)
            y = y_ref[first : first + GROUP, cols]
            offs = offs_ref[first : first + GROUP, cols]
            parts = [y, cos_ref[first : first + GROUP, cols] * y, sin_ref[first : first + GROUP, cols] * y]
            values = jnp.concatenate(parts, axis=0)
            high = values.astype(jnp.bfloat16)
            rest = values - high.astype(jnp.float32)
            mid = rest.astype(jnp.bfloat16)
            low = (rest - mid.astype(jnp.float32)).astype(jnp.bfloat16)
            zero = jnp.zeros((1, tile), jnp.bfloat16)
            for i in range(GROUP):
                upper = offs[i : i + 1] >= half
                pieces = [piece[s * GROUP + i : s * GROUP + i + 1] for piece in (high, mid, low) for s in range(3)]
                stack = jnp.concatenate(
                    [jnp.where(upper, zero, r) for r in pieces]
                    + [jnp.where(upper, r, zero) for r in pieces]
                    + [jnp.zeros((32 - 18, tile), jnp.bfloat16)],
                    axis=0,
                )
                hot = ((offs[i : i + 1] % half) == pix).astype(jnp.bfloat16)
                res = lax.dot_general(
                    stack, hot, (((1,), (1,)), ((), ())), preferred_element_type=jnp.float32
                )
                below = res[0:3] + res[3:6] + res[6:9]
                above = res[9:12] + res[12:15] + res[15:18]
                total = jnp.concatenate([below, above], axis=1)
                h = slot_ref[(first + i) * blocks + blk]
                row = h // slots
                lane = pl.multiple_of((h % slots) * (3 * tile), 128)
                for s in range(3):
                    spot = (pl.ds(row, 1), pl.ds(lane + s * tile, tile))
                    out_ref[spot] = out_ref[spot] + total[s : s + 1]
            return carry

        lax.fori_loop(0, blocks, body, 0)


def bin_call(slot_ids, offs, y, cos, sin, hit_total, tile, slots):
    return pl.pallas_call(
        functools.partial(bin_kernel, slots=slots),
        out_shape=jax.ShapeDtypeStruct((hit_total // slots, slots * 3 * tile), jnp.float32),
        grid_spec=pltpu.PrefetchScalarGridSpec(
            num_scalar_prefetch=1,
            grid=(1,),
            in_specs=[pl.BlockSpec(memory_space=pltpu.VMEM)] * 4,
            out_specs=pl.BlockSpec(memory_space=pltpu.VMEM),
        ),
    )(slot_ids, offs, y, cos, sin)


def read_kernel(slot_ref, maps_ref, offs_ref, cos_ref, sin_ref, out_ref):
    lanes = 128
    dets, samples = offs_ref.shape
    blocks = slot_ref.shape[0] // dets
    tile = maps_ref.shape[1] // 3

    for first in range(0, dets, GROUP):
        def body(blk, carry):
            rows = jnp.concatenate(
                [maps_ref[pl.ds(slot_ref[(first + i) * blocks + blk], 1), :] for i in range(GROUP)],
                axis=0,
            )
            for j in range(tile // lanes):
                start = pl.multiple_of(blk * tile + j * lanes, lanes)
                cols = pl.ds(start, lanes)
                idx = offs_ref[first : first + GROUP, cols]
                low = idx % lanes
                upper = idx >= lanes
                picked = []
                for s in range(3):
                    a = jnp.take_along_axis(
                        rows[:, s * tile : s * tile + lanes], low, axis=1, mode="promise_in_bounds"
                    )
                    b = jnp.take_along_axis(
                        rows[:, s * tile + lanes : (s + 1) * tile], low, axis=1, mode="promise_in_bounds"
                    )
                    picked.append(jnp.where(upper, b, a))
                c = cos_ref[first : first + GROUP, cols]
                sn = sin_ref[first : first + GROUP, cols]
                out_ref[first : first + GROUP, cols] = picked[0] + c * picked[1] + sn * picked[2]
            return carry

        lax.fori_loop(0, blocks, body, 0)


def read_call(slots, maps, offs, cos, sin):
    return pl.pallas_call(
        read_kernel,
        out_shape=jax.ShapeDtypeStruct(offs.shape, jnp.float32),
        grid_spec=pltpu.PrefetchScalarGridSpec(
            num_scalar_prefetch=1,
            grid=(1,),
            in_specs=[pl.BlockSpec(memory_space=pltpu.VMEM)] * 4,
            out_specs=pl.BlockSpec(memory_space=pltpu.VMEM),
        ),
    )(slots, maps, offs, cos, sin)


def local(tod, det_angle, angle_index, offsets, block_slot, hit_tiles, noise_filter, precond):
    shards = lax.axis_size(("tod", "map"))
    hits = hit_tiles[0]
    slot_count = hits.shape[1]
    tiles_dev = precond.shape[0]
    tile_pix = precond.shape[2]
    det_count, samp_count = tod.shape
    blocks_per_det = block_slot.shape[1]
    block_len = samp_count // blocks_per_det
    block_total = det_count * blocks_per_det
    hit_total = shards * slot_count
    highest = lax.Precision.HIGH
    psi = det_angle[:, None] + jnp.pi * angle_index.astype(jnp.float32) / ANGLES
    cosine = jnp.cos(2.0 * psi)
    sine = jnp.sin(2.0 * psi)

    band = noise_filter.shape[1] - 1
    rows = jnp.arange(3 * band, dtype=jnp.int32)[:, None]
    cols = jnp.arange(band, dtype=jnp.int32)[None, :]
    lag = jnp.abs(rows - cols - band)
    lag_hot = (lag[:, :, None] == jnp.arange(band + 1, dtype=jnp.int32)[None, None, :]).astype(
        jnp.float32
    )
    toeplitz = jnp.einsum(
        "dk,rck->drc", noise_filter, lag_hot, precision=highest, preferred_element_type=jnp.float32
    )
    block_count = samp_count // band

    def weigh(stream):
        padded = extended(stream, (("tod", 1),), band).reshape(det_count, block_count + 2, band)
        stacked = jnp.concatenate(
            [padded[:, k : k + block_count] for k in range(3)], axis=2
        )
        out = jnp.einsum(
            "dbj,dji->dbi",
            stacked,
            toeplitz,
            precision=highest,
            preferred_element_type=jnp.float32,
        )
        return out.reshape(det_count, samp_count)

    def owner_sum(arrived, owner_flat, owner_index):
        kept = jnp.where((owner_flat >= 0)[:, None], arrived.reshape(hit_total, 3 * tile_pix), 0.0)
        summed = jnp.zeros((tiles_dev, 3 * tile_pix), jnp.float32).at[owner_index].add(kept)
        return summed

    def binning(stream, partial):
        touched = bin_call(block_slot.reshape(-1), offsets, stream, cosine, sine, hit_total, tile_pix, slot_count)
        arrived, total = exchange(touched.reshape(shards, slot_count * 3 * tile_pix), partial)
        return owner_sum(arrived, owner_flat, owner_index), total

    def projection(field, partial):
        outgoing = jnp.where(
            (owner_flat >= 0)[:, None],
            jnp.take(field, owner_index, axis=0),
            0.0,
        )
        touched, total = exchange(outgoing.reshape(shards, slot_count * 3 * tile_pix), partial)
        stream = read_call(
            block_slot.reshape(-1), touched.reshape(hit_total, 3 * tile_pix), offsets, cosine, sine
        )
        return stream.reshape(det_count, samp_count), total

    touched = bin_call(block_slot.reshape(-1), offsets, weigh(tod), cosine, sine, hit_total, tile_pix, slot_count)
    arrived, _, owner_lists = exchange(
        touched.reshape(shards, slot_count * 3 * tile_pix), None, hits
    )
    owner_flat = owner_lists.reshape(-1)
    owner_index = jnp.clip(owner_flat, 0, tiles_dev - 1)
    rhs = owner_sum(arrived, owner_flat, owner_index)
    solution = jnp.zeros_like(rhs)
    residual = rhs
    zeta = precondition(residual, precond)
    direction = zeta
    stream_dir, norm_now = projection(zeta, jnp.sum(residual * zeta))
    for step in range(ITERS):
        weighed = weigh(stream_dir)
        image, curvature = binning(weighed, jnp.sum(stream_dir * weighed))
        alpha = norm_now / curvature
        solution = solution + alpha * direction
        residual = residual - alpha * image
        if step + 1 < ITERS:
            zeta = precondition(residual, precond)
            stream_zeta, norm_next = projection(zeta, jnp.sum(residual * zeta))
            beta = norm_next / norm_now
            direction = zeta + beta * direction
            stream_dir = stream_zeta + beta * stream_dir
            norm_now = norm_next
    return (solution.reshape(tiles_dev, 3, tile_pix), residual.reshape(tiles_dev, 3, tile_pix))


def solution(mesh):
    in_specs = (
        P("map", "tod"),
        P("map"),
        P("map", "tod"),
        P("map", "tod"),
        P("map", "tod"),
        P(("tod", "map"), None, None),
        P("map", None),
        P(("tod", "map"), None, None),
    )
    out_specs = (P(("tod", "map"), None, None), P(("tod", "map"), None, None))
    return jax.shard_map(local, mesh=mesh, in_specs=in_specs, out_specs=out_specs, check_vma=False)
```

```python
import functools

import jax
import jax.numpy as jnp
from jax import lax
from jax.experimental import pallas as pl
from jax.experimental.pallas import tpu as pltpu
from jax.sharding import PartitionSpec as P

ANGLES = 64
ITERS = 2
SIDE = 128


def extended(cells, sides, width):
    for axis, dim in sides:
        count = lax.axis_size(axis)
        ends = count - 1
        head = lax.slice_in_dim(cells, 0, width, axis=dim)
        tail = lax.slice_in_dim(cells, cells.shape[dim] - width, cells.shape[dim], axis=dim)
        cells = jnp.concatenate(
            [
                lax.ppermute(tail, axis, [(i, (i + 1) % count) for i in range(ends)]),
                cells,
                lax.ppermute(head, axis, [((i + 1) % count, i) for i in range(ends)]),
            ],
            axis=dim,
        )
    return cells


def precondition(field, precond):
    tile = precond.shape[2]
    first, second, third = (field[:, 0:tile], field[:, tile : 2 * tile], field[:, 2 * tile :])
    row_one = precond[:, 0] * first + precond[:, 3] * second + precond[:, 4] * third
    row_two = precond[:, 3] * first + precond[:, 1] * second + precond[:, 5] * third
    row_three = precond[:, 4] * first + precond[:, 5] * second + precond[:, 2] * third
    return jnp.concatenate([row_one, row_two, row_three], axis=1)


def exchange(rows, partial, lists=None):
    shards = rows.shape[0]
    lane = jnp.arange(SIDE, dtype=jnp.int32)[None, :]
    extra = jnp.zeros((shards, SIDE), jnp.float32)
    if partial is not None:
        extra = jnp.where(lane == 0, partial.astype(jnp.float32), extra)
    if lists is not None:
        for k in range(lists.shape[1]):
            extra = jnp.where(lane == 1 + k, lists[:, k : k + 1].astype(jnp.float32), extra)
    rows = jnp.concatenate([rows, extra], axis=1)
    got = lax.all_to_all(rows, ("tod", "map"), split_axis=0, concat_axis=0, tiled=True)
    width = got.shape[1] - SIDE
    total = jnp.sum(got[:, width])
    if lists is None:
        return got[:, :width], total
    arrived_lists = jnp.round(got[:, width + 1 : width + 1 + lists.shape[1]]).astype(jnp.int32)
    return got[:, :width], total, arrived_lists


GROUP = 8


def bin_kernel(slot_ref, offs_ref, y_ref, cos_ref, sin_ref, out_ref, *, slots):
    dets, samples = y_ref.shape
    blocks = slot_ref.shape[0] // dets
    tile = samples // blocks
    out_ref[...] = jnp.zeros(out_ref.shape, out_ref.dtype)
    half = tile // 2
    pix = lax.broadcasted_iota(jnp.int32, (half, tile), 0)

    for first in range(0, dets, GROUP):
        def body(blk, carry):
            start = pl.multiple_of(blk * tile, tile)
            cols = pl.ds(start, tile)
            y = y_ref[first : first + GROUP, cols]
            offs = offs_ref[first : first + GROUP, cols]
            parts = [y, cos_ref[first : first + GROUP, cols] * y, sin_ref[first : first + GROUP, cols] * y]
            values = jnp.concatenate(parts, axis=0)
            high = values.astype(jnp.bfloat16)
            rest = values - high.astype(jnp.float32)
            mid = rest.astype(jnp.bfloat16)
            low = (rest - mid.astype(jnp.float32)).astype(jnp.bfloat16)
            zero = jnp.zeros((1, tile), jnp.bfloat16)
            for i in range(GROUP):
                upper = offs[i : i + 1] >= half
                pieces = [piece[s * GROUP + i : s * GROUP + i + 1] for piece in (high, mid, low) for s in range(3)]
                stack = jnp.concatenate(
                    [jnp.where(upper, zero, r) for r in pieces]
                    + [jnp.where(upper, r, zero) for r in pieces]
                    + [jnp.zeros((32 - 18, tile), jnp.bfloat16)],
                    axis=0,
                )
                hot = ((offs[i : i + 1] % half) == pix).astype(jnp.bfloat16)
                res = lax.dot_general(
                    stack, hot, (((1,), (1,)), ((), ())), preferred_element_type=jnp.float32
                )
                below = res[0:3] + res[3:6] + res[6:9]
                above = res[9:12] + res[12:15] + res[15:18]
                total = jnp.concatenate([below, above], axis=1)
                h = slot_ref[(first + i) * blocks + blk]
                row = h // slots
                lane = pl.multiple_of((h % slots) * (3 * tile), 128)
                for s in range(3):
                    spot = (pl.ds(row, 1), pl.ds(lane + s * tile, tile))
                    out_ref[spot] = out_ref[spot] + total[s : s + 1]
            return carry

        lax.fori_loop(0, blocks, body, 0)


def bin_call(slot_ids, offs, y, cos, sin, hit_total, tile, slots):
    return pl.pallas_call(
        functools.partial(bin_kernel, slots=slots),
        out_shape=jax.ShapeDtypeStruct((hit_total // slots, slots * 3 * tile), jnp.float32),
        grid_spec=pltpu.PrefetchScalarGridSpec(
            num_scalar_prefetch=1,
            grid=(1,),
            in_specs=[pl.BlockSpec(memory_space=pltpu.VMEM)] * 4,
            out_specs=pl.BlockSpec(memory_space=pltpu.VMEM),
        ),
    )(slot_ids, offs, y, cos, sin)


def read_kernel(slot_ref, maps_ref, offs_ref, cos_ref, sin_ref, out_ref):
    lanes = 128
    dets, samples = offs_ref.shape
    blocks = slot_ref.shape[0] // dets
    tile = maps_ref.shape[1] // 3

    for first in range(0, dets, GROUP):
        def body(blk, carry):
            rows = jnp.concatenate(
                [maps_ref[pl.ds(slot_ref[(first + i) * blocks + blk], 1), :] for i in range(GROUP)],
                axis=0,
            )
            for j in range(tile // lanes):
                start = pl.multiple_of(blk * tile + j * lanes, lanes)
                cols = pl.ds(start, lanes)
                idx = offs_ref[first : first + GROUP, cols]
                low = idx % lanes
                upper = idx >= lanes
                picked = []
                for s in range(3):
                    a = jnp.take_along_axis(
                        rows[:, s * tile : s * tile + lanes], low, axis=1, mode="promise_in_bounds"
                    )
                    b = jnp.take_along_axis(
                        rows[:, s * tile + lanes : (s + 1) * tile], low, axis=1, mode="promise_in_bounds"
                    )
                    picked.append(jnp.where(upper, b, a))
                c = cos_ref[first : first + GROUP, cols]
                sn = sin_ref[first : first + GROUP, cols]
                out_ref[first : first + GROUP, cols] = picked[0] + c * picked[1] + sn * picked[2]
            return carry

        lax.fori_loop(0, blocks, body, 0)


def read_call(slots, maps, offs, cos, sin):
    return pl.pallas_call(
        read_kernel,
        out_shape=jax.ShapeDtypeStruct(offs.shape, jnp.float32),
        grid_spec=pltpu.PrefetchScalarGridSpec(
            num_scalar_prefetch=1,
            grid=(1,),
            in_specs=[pl.BlockSpec(memory_space=pltpu.VMEM)] * 4,
            out_specs=pl.BlockSpec(memory_space=pltpu.VMEM),
        ),
    )(slots, maps, offs, cos, sin)


def local(tod, det_angle, angle_index, offsets, block_slot, hit_tiles, noise_filter, precond):
    shards = lax.axis_size(("tod", "map"))
    hits = hit_tiles[0]
    slot_count = hits.shape[1]
    tiles_dev = precond.shape[0]
    tile_pix = precond.shape[2]
    det_count, samp_count = tod.shape
    blocks_per_det = block_slot.shape[1]
    block_len = samp_count // blocks_per_det
    block_total = det_count * blocks_per_det
    hit_total = shards * slot_count
    highest = lax.Precision.HIGH
    psi = det_angle[:, None] + jnp.pi * angle_index.astype(jnp.float32) / ANGLES
    cosine = jnp.cos(2.0 * psi)
    sine = jnp.sin(2.0 * psi)

    band = noise_filter.shape[1] - 1
    rows = jnp.arange(3 * band, dtype=jnp.int32)[:, None]
    cols = jnp.arange(band, dtype=jnp.int32)[None, :]
    lag = jnp.abs(rows - cols - band)
    lag_hot = (lag[:, :, None] == jnp.arange(band + 1, dtype=jnp.int32)[None, None, :]).astype(
        jnp.bfloat16
    )
    taps_high = lax.reduce_precision(noise_filter, exponent_bits=8, mantissa_bits=7)
    taps_rest = noise_filter - taps_high
    taps_mid = lax.reduce_precision(taps_rest, exponent_bits=8, mantissa_bits=7)
    taps_low = lax.reduce_precision(taps_rest - taps_mid, exponent_bits=8, mantissa_bits=7)
    toeplitz = jnp.einsum(
        "pdk,rck->pdrc",
        jnp.stack([taps_high, taps_mid, taps_low]).astype(jnp.bfloat16),
        lag_hot,
        preferred_element_type=jnp.float32,
    ).sum(axis=0)
    block_count = samp_count // band

    def weigh(stream):
        padded = extended(stream, (("tod", 1),), band).reshape(det_count, block_count + 2, band)
        stacked = jnp.concatenate(
            [padded[:, k : k + block_count] for k in range(3)], axis=2
        )
        out = jnp.einsum(
            "dbj,dji->dbi",
            stacked,
            toeplitz,
            precision=highest,
            preferred_element_type=jnp.float32,
        )
        return out.reshape(det_count, samp_count)

    def owner_sum(arrived, owner_flat, owner_index):
        kept = jnp.where((owner_flat >= 0)[:, None], arrived.reshape(hit_total, 3 * tile_pix), 0.0)
        summed = jnp.zeros((tiles_dev, 3 * tile_pix), jnp.float32).at[owner_index].add(kept)
        return summed

    def binning(stream, partial):
        touched = bin_call(block_slot.reshape(-1), offsets, stream, cosine, sine, hit_total, tile_pix, slot_count)
        arrived, total = exchange(touched.reshape(shards, slot_count * 3 * tile_pix), partial)
        return owner_sum(arrived, owner_flat, owner_index), total

    def projection(field, partial):
        outgoing = jnp.where(
            (owner_flat >= 0)[:, None],
            jnp.take(field, owner_index, axis=0),
            0.0,
        )
        touched, total = exchange(outgoing.reshape(shards, slot_count * 3 * tile_pix), partial)
        stream = read_call(
            block_slot.reshape(-1), touched.reshape(hit_total, 3 * tile_pix), offsets, cosine, sine
        )
        return stream.reshape(det_count, samp_count), total

    touched = bin_call(block_slot.reshape(-1), offsets, weigh(tod), cosine, sine, hit_total, tile_pix, slot_count)
    arrived, _, owner_lists = exchange(
        touched.reshape(shards, slot_count * 3 * tile_pix), None, hits
    )
    owner_flat = owner_lists.reshape(-1)
    owner_index = jnp.clip(owner_flat, 0, tiles_dev - 1)
    rhs = owner_sum(arrived, owner_flat, owner_index)
    solution = jnp.zeros_like(rhs)
    residual = rhs
    zeta = precondition(residual, precond)
    direction = zeta
    stream_dir, norm_now = projection(zeta, jnp.sum(residual * zeta))
    for step in range(ITERS):
        weighed = weigh(stream_dir)
        image, curvature = binning(weighed, jnp.sum(stream_dir * weighed))
        alpha = norm_now / curvature
        solution = solution + alpha * direction
        residual = residual - alpha * image
        if step + 1 < ITERS:
            zeta = precondition(residual, precond)
            stream_zeta, norm_next = projection(zeta, jnp.sum(residual * zeta))
            beta = norm_next / norm_now
            direction = zeta + beta * direction
            stream_dir = stream_zeta + beta * stream_dir
            norm_now = norm_next
    return (solution.reshape(tiles_dev, 3, tile_pix), residual.reshape(tiles_dev, 3, tile_pix))


def solution(mesh):
    in_specs = (
        P("map", "tod"),
        P("map"),
        P("map", "tod"),
        P("map", "tod"),
        P("map", "tod"),
        P(("tod", "map"), None, None),
        P("map", None),
        P(("tod", "map"), None, None),
    )
    out_specs = (P(("tod", "map"), None, None), P(("tod", "map"), None, None))
    return jax.shard_map(local, mesh=mesh, in_specs=in_specs, out_specs=out_specs, check_vma=False)
```

```python
import functools

import jax
import jax.numpy as jnp
from jax import lax
from jax.experimental import pallas as pl
from jax.experimental.pallas import tpu as pltpu
from jax.sharding import PartitionSpec as P

ANGLES = 64
ITERS = 2
SIDE = 128


def extended(cells, sides, width):
    for axis, dim in sides:
        count = lax.axis_size(axis)
        ends = count - 1
        head = lax.slice_in_dim(cells, 0, width, axis=dim)
        tail = lax.slice_in_dim(cells, cells.shape[dim] - width, cells.shape[dim], axis=dim)
        cells = jnp.concatenate(
            [
                lax.ppermute(tail, axis, [(i, (i + 1) % count) for i in range(ends)]),
                cells,
                lax.ppermute(head, axis, [((i + 1) % count, i) for i in range(ends)]),
            ],
            axis=dim,
        )
    return cells


def precondition(field, precond):
    tile = precond.shape[2]
    first, second, third = (field[:, 0:tile], field[:, tile : 2 * tile], field[:, 2 * tile :])
    row_one = precond[:, 0] * first + precond[:, 3] * second + precond[:, 4] * third
    row_two = precond[:, 3] * first + precond[:, 1] * second + precond[:, 5] * third
    row_three = precond[:, 4] * first + precond[:, 5] * second + precond[:, 2] * third
    return jnp.concatenate([row_one, row_two, row_three], axis=1)


def exchange(rows, partial, lists=None):
    shards = rows.shape[0]
    lane = jnp.arange(SIDE, dtype=jnp.int32)[None, :]
    extra = jnp.zeros((shards, SIDE), jnp.float32)
    if partial is not None:
        extra = jnp.where(lane == 0, partial.astype(jnp.float32), extra)
    if lists is not None:
        for k in range(lists.shape[1]):
            extra = jnp.where(lane == 1 + k, lists[:, k : k + 1].astype(jnp.float32), extra)
    rows = jnp.concatenate([rows, extra], axis=1)
    got = lax.all_to_all(rows, ("tod", "map"), split_axis=0, concat_axis=0, tiled=True)
    width = got.shape[1] - SIDE
    total = jnp.sum(got[:, width])
    if lists is None:
        return got[:, :width], total
    arrived_lists = jnp.round(got[:, width + 1 : width + 1 + lists.shape[1]]).astype(jnp.int32)
    return got[:, :width], total, arrived_lists


GROUP = 8


def bin_kernel(slot_ref, offs_ref, y_ref, cos_ref, sin_ref, out_ref, *, slots):
    dets, samples = y_ref.shape
    blocks = slot_ref.shape[0] // dets
    tile = samples // blocks
    out_ref[...] = jnp.zeros(out_ref.shape, out_ref.dtype)
    half = tile // 2
    pix = lax.broadcasted_iota(jnp.int32, (half, tile), 0)

    for first in range(0, dets, GROUP):
        def body(blk, carry):
            start = pl.multiple_of(blk * tile, tile)
            cols = pl.ds(start, tile)
            y = y_ref[first : first + GROUP, cols]
            offs = offs_ref[first : first + GROUP, cols]
            parts = [y, cos_ref[first : first + GROUP, cols] * y, sin_ref[first : first + GROUP, cols] * y]
            values = jnp.concatenate(parts, axis=0)
            high = values.astype(jnp.bfloat16)
            rest = values - high.astype(jnp.float32)
            mid = rest.astype(jnp.bfloat16)
            low = (rest - mid.astype(jnp.float32)).astype(jnp.bfloat16)
            zero = jnp.zeros((1, tile), jnp.bfloat16)
            for i in range(GROUP):
                upper = offs[i : i + 1] >= half
                pieces = [piece[s * GROUP + i : s * GROUP + i + 1] for piece in (high, mid, low) for s in range(3)]
                stack = jnp.concatenate(
                    [jnp.where(upper, zero, r) for r in pieces]
                    + [jnp.where(upper, r, zero) for r in pieces]
                    + [jnp.zeros((32 - 18, tile), jnp.bfloat16)],
                    axis=0,
                )
                hot = ((offs[i : i + 1] % half) == pix).astype(jnp.bfloat16)
                res = lax.dot_general(
                    stack, hot, (((1,), (1,)), ((), ())), preferred_element_type=jnp.float32
                )
                below = res[0:3] + res[3:6] + res[6:9]
                above = res[9:12] + res[12:15] + res[15:18]
                total = jnp.concatenate([below, above], axis=1)
                h = slot_ref[(first + i) * blocks + blk]
                row = h // slots
                lane = pl.multiple_of((h % slots) * (3 * tile), 128)
                for s in range(3):
                    spot = (pl.ds(row, 1), pl.ds(lane + s * tile, tile))
                    out_ref[spot] = out_ref[spot] + total[s : s + 1]
            return carry

        lax.fori_loop(0, blocks, body, 0)


def bin_call(slot_ids, offs, y, cos, sin, hit_total, tile, slots):
    return pl.pallas_call(
        functools.partial(bin_kernel, slots=slots),
        out_shape=jax.ShapeDtypeStruct((hit_total // slots, slots * 3 * tile), jnp.float32),
        grid_spec=pltpu.PrefetchScalarGridSpec(
            num_scalar_prefetch=1,
            grid=(1,),
            in_specs=[pl.BlockSpec(memory_space=pltpu.VMEM)] * 4,
            out_specs=pl.BlockSpec(memory_space=pltpu.VMEM),
        ),
    )(slot_ids, offs, y, cos, sin)


def read_kernel(slot_ref, maps_ref, offs_ref, cos_ref, sin_ref, out_ref):
    lanes = 128
    dets, samples = offs_ref.shape
    blocks = slot_ref.shape[0] // dets
    tile = maps_ref.shape[1] // 3

    for first in range(0, dets, GROUP):
        def body(blk, carry):
            rows = jnp.concatenate(
                [maps_ref[pl.ds(slot_ref[(first + i) * blocks + blk], 1), :] for i in range(GROUP)],
                axis=0,
            )
            for j in range(tile // lanes):
                start = pl.multiple_of(blk * tile + j * lanes, lanes)
                cols = pl.ds(start, lanes)
                idx = offs_ref[first : first + GROUP, cols]
                low = idx % lanes
                upper = idx >= lanes
                picked = []
                for s in range(3):
                    a = jnp.take_along_axis(
                        rows[:, s * tile : s * tile + lanes], low, axis=1, mode="promise_in_bounds"
                    )
                    b = jnp.take_along_axis(
                        rows[:, s * tile + lanes : (s + 1) * tile], low, axis=1, mode="promise_in_bounds"
                    )
                    picked.append(jnp.where(upper, b, a))
                c = cos_ref[first : first + GROUP, cols]
                sn = sin_ref[first : first + GROUP, cols]
                out_ref[first : first + GROUP, cols] = picked[0] + c * picked[1] + sn * picked[2]
            return carry

        lax.fori_loop(0, blocks, body, 0)


def read_call(slots, maps, offs, cos, sin):
    return pl.pallas_call(
        read_kernel,
        out_shape=jax.ShapeDtypeStruct(offs.shape, jnp.float32),
        grid_spec=pltpu.PrefetchScalarGridSpec(
            num_scalar_prefetch=1,
            grid=(1,),
            in_specs=[pl.BlockSpec(memory_space=pltpu.VMEM)] * 4,
            out_specs=pl.BlockSpec(memory_space=pltpu.VMEM),
        ),
    )(slots, maps, offs, cos, sin)


def local(tod, det_angle, angle_index, offsets, block_slot, hit_tiles, noise_filter, precond):
    shards = lax.axis_size(("tod", "map"))
    hits = hit_tiles[0]
    slot_count = hits.shape[1]
    tiles_dev = precond.shape[0]
    tile_pix = precond.shape[2]
    det_count, samp_count = tod.shape
    blocks_per_det = block_slot.shape[1]
    block_len = samp_count // blocks_per_det
    block_total = det_count * blocks_per_det
    hit_total = shards * slot_count
    highest = lax.Precision.HIGH
    psi = det_angle[:, None] + jnp.pi * angle_index.astype(jnp.float32) / ANGLES
    cosine = jnp.cos(2.0 * psi)
    sine = jnp.sin(2.0 * psi)

    band = noise_filter.shape[1] - 1
    rows = jnp.arange(3 * band, dtype=jnp.int32)[:, None]
    cols = jnp.arange(band, dtype=jnp.int32)[None, :]
    lag = jnp.abs(rows - cols - band)
    lag_hot = (lag[:, :, None] == jnp.arange(band + 1, dtype=jnp.int32)[None, None, :]).astype(
        jnp.bfloat16
    )
    taps_high = lax.reduce_precision(noise_filter, exponent_bits=8, mantissa_bits=7)
    taps_rest = noise_filter - taps_high
    taps_mid = lax.reduce_precision(taps_rest, exponent_bits=8, mantissa_bits=7)
    taps_low = lax.reduce_precision(taps_rest - taps_mid, exponent_bits=8, mantissa_bits=7)
    toeplitz = jnp.einsum(
        "pdk,rck->pdrc",
        jnp.stack([taps_high, taps_mid, taps_low]).astype(jnp.bfloat16),
        lag_hot,
        preferred_element_type=jnp.float32,
    ).sum(axis=0)
    block_count = samp_count // band

    def weigh(stream):
        padded = extended(stream, (("tod", 1),), band).reshape(det_count, block_count + 2, band)
        stacked = jnp.concatenate(
            [padded[:, k : k + block_count] for k in range(3)], axis=2
        )
        out = jnp.einsum(
            "dbj,dji->dbi",
            stacked,
            toeplitz,
            precision=highest,
            preferred_element_type=jnp.float32,
        )
        return out.reshape(det_count, samp_count)

    def owner_sum(arrived, owner_flat, owner_index):
        placement = (
            owner_flat[:, None] == jnp.arange(tiles_dev, dtype=jnp.int32)[None, :]
        ).astype(jnp.float32)
        return lax.dot_general(
            placement,
            arrived.reshape(hit_total, 3 * tile_pix),
            (((0,), (0,)), ((), ())),
            precision=highest,
            preferred_element_type=jnp.float32,
        )

    def binning(stream, partial):
        touched = bin_call(block_slot.reshape(-1), offsets, stream, cosine, sine, hit_total, tile_pix, slot_count)
        arrived, total = exchange(touched.reshape(shards, slot_count * 3 * tile_pix), partial)
        return owner_sum(arrived, owner_flat, owner_index), total

    def projection(field, partial):
        outgoing = jnp.where(
            (owner_flat >= 0)[:, None],
            jnp.take(field, owner_index, axis=0),
            0.0,
        )
        touched, total = exchange(outgoing.reshape(shards, slot_count * 3 * tile_pix), partial)
        stream = read_call(
            block_slot.reshape(-1), touched.reshape(hit_total, 3 * tile_pix), offsets, cosine, sine
        )
        return stream.reshape(det_count, samp_count), total

    touched = bin_call(block_slot.reshape(-1), offsets, weigh(tod), cosine, sine, hit_total, tile_pix, slot_count)
    arrived, _, owner_lists = exchange(
        touched.reshape(shards, slot_count * 3 * tile_pix), None, hits
    )
    owner_flat = owner_lists.reshape(-1)
    owner_index = jnp.clip(owner_flat, 0, tiles_dev - 1)
    rhs = owner_sum(arrived, owner_flat, owner_index)
    solution = jnp.zeros_like(rhs)
    residual = rhs
    zeta = precondition(residual, precond)
    direction = zeta
    stream_dir, norm_now = projection(zeta, jnp.sum(residual * zeta))
    for step in range(ITERS):
        weighed = weigh(stream_dir)
        image, curvature = binning(weighed, jnp.sum(stream_dir * weighed))
        alpha = norm_now / curvature
        solution = solution + alpha * direction
        residual = residual - alpha * image
        if step + 1 < ITERS:
            zeta = precondition(residual, precond)
            stream_zeta, norm_next = projection(zeta, jnp.sum(residual * zeta))
            beta = norm_next / norm_now
            direction = zeta + beta * direction
            stream_dir = stream_zeta + beta * stream_dir
            norm_now = norm_next
    return (solution.reshape(tiles_dev, 3, tile_pix), residual.reshape(tiles_dev, 3, tile_pix))


def solution(mesh):
    in_specs = (
        P("map", "tod"),
        P("map"),
        P("map", "tod"),
        P("map", "tod"),
        P("map", "tod"),
        P(("tod", "map"), None, None),
        P("map", None),
        P(("tod", "map"), None, None),
    )
    out_specs = (P(("tod", "map"), None, None), P(("tod", "map"), None, None))
    return jax.shard_map(local, mesh=mesh, in_specs=in_specs, out_specs=out_specs, check_vma=False)
```

```python
import functools

import jax
import jax.numpy as jnp
from jax import lax
from jax.experimental import pallas as pl
from jax.experimental.pallas import tpu as pltpu
from jax.sharding import PartitionSpec as P

ANGLES = 64
ITERS = 2
SIDE = 128


def extended(cells, sides, width):
    for axis, dim in sides:
        count = lax.axis_size(axis)
        ends = count - 1
        head = lax.slice_in_dim(cells, 0, width, axis=dim)
        tail = lax.slice_in_dim(cells, cells.shape[dim] - width, cells.shape[dim], axis=dim)
        cells = jnp.concatenate(
            [
                lax.ppermute(tail, axis, [(i, (i + 1) % count) for i in range(ends)]),
                cells,
                lax.ppermute(head, axis, [((i + 1) % count, i) for i in range(ends)]),
            ],
            axis=dim,
        )
    return cells


def precondition(field, precond):
    tile = precond.shape[2]
    first, second, third = (field[:, 0:tile], field[:, tile : 2 * tile], field[:, 2 * tile :])
    row_one = precond[:, 0] * first + precond[:, 3] * second + precond[:, 4] * third
    row_two = precond[:, 3] * first + precond[:, 1] * second + precond[:, 5] * third
    row_three = precond[:, 4] * first + precond[:, 5] * second + precond[:, 2] * third
    return jnp.concatenate([row_one, row_two, row_three], axis=1)


def exchange(rows, partial, lists=None):
    shards = rows.shape[0]
    lane = jnp.arange(SIDE, dtype=jnp.int32)[None, :]
    extra = jnp.zeros((shards, SIDE), jnp.float32)
    if partial is not None:
        extra = jnp.where(lane == 0, partial.astype(jnp.float32), extra)
    if lists is not None:
        for k in range(lists.shape[1]):
            extra = jnp.where(lane == 1 + k, lists[:, k : k + 1].astype(jnp.float32), extra)
    rows = jnp.concatenate([rows, extra], axis=1)
    got = lax.all_to_all(rows, ("tod", "map"), split_axis=0, concat_axis=0, tiled=True)
    width = got.shape[1] - SIDE
    total = jnp.sum(got[:, width])
    if lists is None:
        return got[:, :width], total
    arrived_lists = jnp.round(got[:, width + 1 : width + 1 + lists.shape[1]]).astype(jnp.int32)
    return got[:, :width], total, arrived_lists


GROUP = 8


def bin_kernel(slot_ref, offs_ref, y_ref, cos_ref, sin_ref, out_ref, *, slots):
    dets, samples = y_ref.shape
    blocks = slot_ref.shape[0] // dets
    tile = samples // blocks
    out_ref[...] = jnp.zeros(out_ref.shape, out_ref.dtype)
    half = tile // 2
    pix = lax.broadcasted_iota(jnp.int32, (half, tile), 0)

    for first in range(0, dets, GROUP):
        def body(blk, carry):
            start = pl.multiple_of(blk * tile, tile)
            cols = pl.ds(start, tile)
            y = y_ref[first : first + GROUP, cols]
            offs = offs_ref[first : first + GROUP, cols]
            parts = [y, cos_ref[first : first + GROUP, cols] * y, sin_ref[first : first + GROUP, cols] * y]
            values = jnp.concatenate(parts, axis=0)
            high = values.astype(jnp.bfloat16)
            rest = values - high.astype(jnp.float32)
            mid = rest.astype(jnp.bfloat16)
            low = (rest - mid.astype(jnp.float32)).astype(jnp.bfloat16)
            zero = jnp.zeros((1, tile), jnp.bfloat16)
            for i in range(GROUP):
                upper = offs[i : i + 1] >= half
                pieces = [piece[s * GROUP + i : s * GROUP + i + 1] for piece in (high, mid, low) for s in range(3)]
                stack = jnp.concatenate(
                    [jnp.where(upper, zero, r) for r in pieces]
                    + [jnp.where(upper, r, zero) for r in pieces]
                    + [jnp.zeros((32 - 18, tile), jnp.bfloat16)],
                    axis=0,
                )
                hot = ((offs[i : i + 1] % half) == pix).astype(jnp.bfloat16)
                res = lax.dot_general(
                    stack, hot, (((1,), (1,)), ((), ())), preferred_element_type=jnp.float32
                )
                below = res[0:3] + res[3:6] + res[6:9]
                above = res[9:12] + res[12:15] + res[15:18]
                total = jnp.concatenate([below, above], axis=1)
                h = slot_ref[(first + i) * blocks + blk]
                row = h // slots
                lane = pl.multiple_of((h % slots) * (3 * tile), 128)
                for s in range(3):
                    spot = (pl.ds(row, 1), pl.ds(lane + s * tile, tile))
                    out_ref[spot] = out_ref[spot] + total[s : s + 1]
            return carry

        lax.fori_loop(0, blocks, body, 0)


def bin_call(slot_ids, offs, y, cos, sin, hit_total, tile, slots):
    return pl.pallas_call(
        functools.partial(bin_kernel, slots=slots),
        out_shape=jax.ShapeDtypeStruct((hit_total // slots, slots * 3 * tile), jnp.float32),
        grid_spec=pltpu.PrefetchScalarGridSpec(
            num_scalar_prefetch=1,
            grid=(1,),
            in_specs=[pl.BlockSpec(memory_space=pltpu.VMEM)] * 4,
            out_specs=pl.BlockSpec(memory_space=pltpu.VMEM),
        ),
    )(slot_ids, offs, y, cos, sin)


def read_kernel(slot_ref, maps_ref, offs_ref, cos_ref, sin_ref, out_ref):
    lanes = 128
    dets, samples = offs_ref.shape
    blocks = slot_ref.shape[0] // dets
    tile = maps_ref.shape[1] // 3

    for first in range(0, dets, GROUP):
        def body(blk, carry):
            rows = jnp.concatenate(
                [maps_ref[pl.ds(slot_ref[(first + i) * blocks + blk], 1), :] for i in range(GROUP)],
                axis=0,
            )
            for j in range(tile // lanes):
                start = pl.multiple_of(blk * tile + j * lanes, lanes)
                cols = pl.ds(start, lanes)
                idx = offs_ref[first : first + GROUP, cols]
                low = idx % lanes
                upper = idx >= lanes
                picked = []
                for s in range(3):
                    a = jnp.take_along_axis(
                        rows[:, s * tile : s * tile + lanes], low, axis=1, mode="promise_in_bounds"
                    )
                    b = jnp.take_along_axis(
                        rows[:, s * tile + lanes : (s + 1) * tile], low, axis=1, mode="promise_in_bounds"
                    )
                    picked.append(jnp.where(upper, b, a))
                c = cos_ref[first : first + GROUP, cols]
                sn = sin_ref[first : first + GROUP, cols]
                out_ref[first : first + GROUP, cols] = picked[0] + c * picked[1] + sn * picked[2]
            return carry

        lax.fori_loop(0, blocks, body, 0)


def read_call(slots, maps, offs, cos, sin):
    return pl.pallas_call(
        read_kernel,
        out_shape=jax.ShapeDtypeStruct(offs.shape, jnp.float32),
        grid_spec=pltpu.PrefetchScalarGridSpec(
            num_scalar_prefetch=1,
            grid=(1,),
            in_specs=[pl.BlockSpec(memory_space=pltpu.VMEM)] * 4,
            out_specs=pl.BlockSpec(memory_space=pltpu.VMEM),
        ),
    )(slots, maps, offs, cos, sin)


def local(tod, det_angle, angle_index, offsets, block_slot, hit_tiles, noise_filter, precond):
    shards = lax.axis_size(("tod", "map"))
    hits = hit_tiles[0]
    slot_count = hits.shape[1]
    tiles_dev = precond.shape[0]
    tile_pix = precond.shape[2]
    det_count, samp_count = tod.shape
    blocks_per_det = block_slot.shape[1]
    block_len = samp_count // blocks_per_det
    block_total = det_count * blocks_per_det
    hit_total = shards * slot_count
    highest = lax.Precision.HIGH
    psi = det_angle[:, None] + jnp.pi * angle_index.astype(jnp.float32) / ANGLES
    cosine = jnp.cos(2.0 * psi)
    sine = jnp.sin(2.0 * psi)

    band = noise_filter.shape[1] - 1
    rows = jnp.arange(3 * band, dtype=jnp.int32)[:, None]
    cols = jnp.arange(band, dtype=jnp.int32)[None, :]
    lag = jnp.abs(rows - cols - band)
    lag_hot = (lag[:, :, None] == jnp.arange(band + 1, dtype=jnp.int32)[None, None, :]).astype(
        jnp.bfloat16
    )
    taps_high = lax.reduce_precision(noise_filter, exponent_bits=8, mantissa_bits=7)
    taps_rest = noise_filter - taps_high
    taps_mid = lax.reduce_precision(taps_rest, exponent_bits=8, mantissa_bits=7)
    taps_low = lax.reduce_precision(taps_rest - taps_mid, exponent_bits=8, mantissa_bits=7)
    toeplitz = jnp.einsum(
        "pdk,rck->pdrc",
        jnp.stack([taps_high, taps_mid, taps_low]).astype(jnp.bfloat16),
        lag_hot,
        preferred_element_type=jnp.float32,
    ).sum(axis=0)
    block_count = samp_count // band

    def weigh(stream):
        padded = extended(stream, (("tod", 1),), band).reshape(det_count, block_count + 2, band)
        stacked = jnp.concatenate(
            [padded[:, k : k + block_count] for k in range(3)], axis=2
        )
        out = jnp.einsum(
            "dbj,dji->dbi",
            stacked,
            toeplitz,
            precision=highest,
            preferred_element_type=jnp.float32,
        )
        return out.reshape(det_count, samp_count)

    def owner_sum(arrived, owner_flat, owner_index):
        width = 3 * tile_pix
        lists = owner_flat.reshape(shards, slot_count)
        summed = None
        for j in range(slot_count):
            placement = (
                lists[:, j : j + 1] == jnp.arange(tiles_dev, dtype=jnp.int32)[None, :]
            ).astype(jnp.float32)
            part = lax.dot_general(
                placement,
                arrived[:, j * width : (j + 1) * width],
                (((0,), (0,)), ((), ())),
                precision=highest,
                preferred_element_type=jnp.float32,
            )
            summed = part if summed is None else summed + part
        return summed

    def binning(stream, partial):
        touched = bin_call(block_slot.reshape(-1), offsets, stream, cosine, sine, hit_total, tile_pix, slot_count)
        arrived, total = exchange(touched.reshape(shards, slot_count * 3 * tile_pix), partial)
        return owner_sum(arrived, owner_flat, owner_index), total

    def projection(field, partial):
        outgoing = jnp.where(
            (owner_flat >= 0)[:, None],
            jnp.take(field, owner_index, axis=0),
            0.0,
        )
        touched, total = exchange(outgoing.reshape(shards, slot_count * 3 * tile_pix), partial)
        stream = read_call(
            block_slot.reshape(-1), touched.reshape(hit_total, 3 * tile_pix), offsets, cosine, sine
        )
        return stream.reshape(det_count, samp_count), total

    touched = bin_call(block_slot.reshape(-1), offsets, weigh(tod), cosine, sine, hit_total, tile_pix, slot_count)
    arrived, _, owner_lists = exchange(
        touched.reshape(shards, slot_count * 3 * tile_pix), None, hits
    )
    owner_flat = owner_lists.reshape(-1)
    owner_index = jnp.clip(owner_flat, 0, tiles_dev - 1)
    rhs = owner_sum(arrived, owner_flat, owner_index)
    solution = jnp.zeros_like(rhs)
    residual = rhs
    zeta = precondition(residual, precond)
    direction = zeta
    stream_dir, norm_now = projection(zeta, jnp.sum(residual * zeta))
    for step in range(ITERS):
        weighed = weigh(stream_dir)
        image, curvature = binning(weighed, jnp.sum(stream_dir * weighed))
        alpha = norm_now / curvature
        solution = solution + alpha * direction
        residual = residual - alpha * image
        if step + 1 < ITERS:
            zeta = precondition(residual, precond)
            stream_zeta, norm_next = projection(zeta, jnp.sum(residual * zeta))
            beta = norm_next / norm_now
            direction = zeta + beta * direction
            stream_dir = stream_zeta + beta * stream_dir
            norm_now = norm_next
    return (solution.reshape(tiles_dev, 3, tile_pix), residual.reshape(tiles_dev, 3, tile_pix))


def solution(mesh):
    in_specs = (
        P("map", "tod"),
        P("map"),
        P("map", "tod"),
        P("map", "tod"),
        P("map", "tod"),
        P(("tod", "map"), None, None),
        P("map", None),
        P(("tod", "map"), None, None),
    )
    out_specs = (P(("tod", "map"), None, None), P(("tod", "map"), None, None))
    return jax.shard_map(local, mesh=mesh, in_specs=in_specs, out_specs=out_specs, check_vma=False)
```

```python
import functools

import jax
import jax.numpy as jnp
from jax import lax
from jax.experimental import pallas as pl
from jax.experimental.pallas import tpu as pltpu
from jax.sharding import PartitionSpec as P

ANGLES = 64
ITERS = 2
SIDE = 128


def extended(cells, sides, width):
    for axis, dim in sides:
        count = lax.axis_size(axis)
        ends = count - 1
        head = lax.slice_in_dim(cells, 0, width, axis=dim)
        tail = lax.slice_in_dim(cells, cells.shape[dim] - width, cells.shape[dim], axis=dim)
        cells = jnp.concatenate(
            [
                lax.ppermute(tail, axis, [(i, (i + 1) % count) for i in range(ends)]),
                cells,
                lax.ppermute(head, axis, [((i + 1) % count, i) for i in range(ends)]),
            ],
            axis=dim,
        )
    return cells


def precondition(field, precond):
    tile = precond.shape[2]
    first, second, third = (field[:, 0:tile], field[:, tile : 2 * tile], field[:, 2 * tile :])
    row_one = precond[:, 0] * first + precond[:, 3] * second + precond[:, 4] * third
    row_two = precond[:, 3] * first + precond[:, 1] * second + precond[:, 5] * third
    row_three = precond[:, 4] * first + precond[:, 5] * second + precond[:, 2] * third
    return jnp.concatenate([row_one, row_two, row_three], axis=1)


def exchange(rows, partial, lists=None):
    shards = rows.shape[0]
    lane = jnp.arange(SIDE, dtype=jnp.int32)[None, :]
    extra = jnp.zeros((shards, SIDE), jnp.float32)
    if partial is not None:
        extra = jnp.where(lane == 0, partial.astype(jnp.float32), extra)
    if lists is not None:
        for k in range(lists.shape[1]):
            extra = jnp.where(lane == 1 + k, lists[:, k : k + 1].astype(jnp.float32), extra)
    rows = jnp.concatenate([rows, extra], axis=1)
    got = lax.all_to_all(rows, ("tod", "map"), split_axis=0, concat_axis=0, tiled=True)
    width = got.shape[1] - SIDE
    total = jnp.sum(got[:, width])
    if lists is None:
        return got[:, :width], total
    arrived_lists = jnp.round(got[:, width + 1 : width + 1 + lists.shape[1]]).astype(jnp.int32)
    return got[:, :width], total, arrived_lists


GROUP = 8


def bin_kernel(slot_ref, offs_ref, y_ref, cos_ref, sin_ref, out_ref, *, slots):
    dets, samples = y_ref.shape
    blocks = slot_ref.shape[0] // dets
    tile = samples // blocks
    out_ref[...] = jnp.zeros(out_ref.shape, out_ref.dtype)
    half = tile // 2
    pix = lax.broadcasted_iota(jnp.int32, (half, tile), 0)

    for first in range(0, dets, GROUP):
        def body(blk, carry):
            start = pl.multiple_of(blk * tile, tile)
            cols = pl.ds(start, tile)
            y = y_ref[first : first + GROUP, cols]
            offs = offs_ref[first : first + GROUP, cols]
            parts = [y, cos_ref[first : first + GROUP, cols] * y, sin_ref[first : first + GROUP, cols] * y]
            values = jnp.concatenate(parts, axis=0)
            high = values.astype(jnp.bfloat16)
            rest = values - high.astype(jnp.float32)
            mid = rest.astype(jnp.bfloat16)
            low = (rest - mid.astype(jnp.float32)).astype(jnp.bfloat16)
            zero = jnp.zeros((1, tile), jnp.bfloat16)
            for i in range(GROUP):
                upper = offs[i : i + 1] >= half
                pieces = [piece[s * GROUP + i : s * GROUP + i + 1] for piece in (high, mid, low) for s in range(3)]
                stack = jnp.concatenate(
                    [jnp.where(upper, zero, r) for r in pieces]
                    + [jnp.where(upper, r, zero) for r in pieces]
                    + [jnp.zeros((32 - 18, tile), jnp.bfloat16)],
                    axis=0,
                )
                hot = ((offs[i : i + 1] % half) == pix).astype(jnp.bfloat16)
                res = lax.dot_general(
                    stack, hot, (((1,), (1,)), ((), ())), preferred_element_type=jnp.float32
                )
                below = res[0:3] + res[3:6] + res[6:9]
                above = res[9:12] + res[12:15] + res[15:18]
                total = jnp.concatenate([below, above], axis=1)
                h = slot_ref[(first + i) * blocks + blk]
                row = h // slots
                lane = pl.multiple_of((h % slots) * (3 * tile), 128)
                for s in range(3):
                    spot = (pl.ds(row, 1), pl.ds(lane + s * tile, tile))
                    out_ref[spot] = out_ref[spot] + total[s : s + 1]
            return carry

        lax.fori_loop(0, blocks, body, 0)


def bin_call(slot_ids, offs, y, cos, sin, hit_total, tile, slots):
    return pl.pallas_call(
        functools.partial(bin_kernel, slots=slots),
        out_shape=jax.ShapeDtypeStruct((hit_total // slots, slots * 3 * tile), jnp.float32),
        grid_spec=pltpu.PrefetchScalarGridSpec(
            num_scalar_prefetch=1,
            grid=(1,),
            in_specs=[pl.BlockSpec(memory_space=pltpu.VMEM)] * 4,
            out_specs=pl.BlockSpec(memory_space=pltpu.VMEM),
        ),
    )(slot_ids, offs, y, cos, sin)


def read_kernel(slot_ref, maps_ref, offs_ref, cos_ref, sin_ref, out_ref):
    lanes = 128
    dets, samples = offs_ref.shape
    blocks = slot_ref.shape[0] // dets
    tile = maps_ref.shape[1] // 3

    for first in range(0, dets, GROUP):
        def body(blk, carry):
            rows = jnp.concatenate(
                [maps_ref[pl.ds(slot_ref[(first + i) * blocks + blk], 1), :] for i in range(GROUP)],
                axis=0,
            )
            for j in range(tile // lanes):
                start = pl.multiple_of(blk * tile + j * lanes, lanes)
                cols = pl.ds(start, lanes)
                idx = offs_ref[first : first + GROUP, cols]
                low = idx % lanes
                upper = idx >= lanes
                picked = []
                for s in range(3):
                    a = jnp.take_along_axis(
                        rows[:, s * tile : s * tile + lanes], low, axis=1, mode="promise_in_bounds"
                    )
                    b = jnp.take_along_axis(
                        rows[:, s * tile + lanes : (s + 1) * tile], low, axis=1, mode="promise_in_bounds"
                    )
                    picked.append(jnp.where(upper, b, a))
                c = cos_ref[first : first + GROUP, cols]
                sn = sin_ref[first : first + GROUP, cols]
                out_ref[first : first + GROUP, cols] = picked[0] + c * picked[1] + sn * picked[2]
            return carry

        lax.fori_loop(0, blocks, body, 0)


def read_call(slots, maps, offs, cos, sin):
    return pl.pallas_call(
        read_kernel,
        out_shape=jax.ShapeDtypeStruct(offs.shape, jnp.float32),
        grid_spec=pltpu.PrefetchScalarGridSpec(
            num_scalar_prefetch=1,
            grid=(1,),
            in_specs=[pl.BlockSpec(memory_space=pltpu.VMEM)] * 4,
            out_specs=pl.BlockSpec(memory_space=pltpu.VMEM),
        ),
    )(slots, maps, offs, cos, sin)


def local(tod, det_angle, angle_index, offsets, block_slot, hit_tiles, noise_filter, precond):
    shards = lax.axis_size(("tod", "map"))
    hits = hit_tiles[0]
    slot_count = hits.shape[1]
    tiles_dev = precond.shape[0]
    tile_pix = precond.shape[2]
    det_count, samp_count = tod.shape
    blocks_per_det = block_slot.shape[1]
    block_len = samp_count // blocks_per_det
    block_total = det_count * blocks_per_det
    hit_total = shards * slot_count
    highest = lax.Precision.HIGH
    psi = det_angle[:, None] + jnp.pi * angle_index.astype(jnp.float32) / ANGLES
    cosine = jnp.cos(2.0 * psi)
    sine = jnp.sin(2.0 * psi)

    band = noise_filter.shape[1] - 1
    rows = jnp.arange(3 * band, dtype=jnp.int32)[:, None]
    cols = jnp.arange(band, dtype=jnp.int32)[None, :]
    lag = jnp.abs(rows - cols - band)
    lag_hot = (lag[:, :, None] == jnp.arange(band + 1, dtype=jnp.int32)[None, None, :]).astype(
        jnp.bfloat16
    )
    taps_high = lax.reduce_precision(noise_filter, exponent_bits=8, mantissa_bits=7)
    taps_rest = noise_filter - taps_high
    taps_mid = lax.reduce_precision(taps_rest, exponent_bits=8, mantissa_bits=7)
    taps_low = lax.reduce_precision(taps_rest - taps_mid, exponent_bits=8, mantissa_bits=7)
    toeplitz = jnp.einsum(
        "pdk,rck->pdrc",
        jnp.stack([taps_high, taps_mid, taps_low]).astype(jnp.bfloat16),
        lag_hot,
        preferred_element_type=jnp.float32,
    ).sum(axis=0)
    block_count = samp_count // band

    def weigh(stream):
        padded = extended(stream, (("tod", 1),), band).reshape(det_count, block_count + 2, band)
        stacked = jnp.concatenate(
            [padded[:, k : k + block_count] for k in range(3)], axis=2
        )
        out = jnp.einsum(
            "dbj,dji->dbi",
            stacked,
            toeplitz,
            precision=highest,
            preferred_element_type=jnp.float32,
        )
        return out.reshape(det_count, samp_count)

    def owner_sum(arrived, owner_flat, owner_index):
        placement = (
            owner_flat[:, None] == jnp.arange(tiles_dev, dtype=jnp.int32)[None, :]
        ).astype(jnp.float32)
        return lax.dot_general(
            placement,
            arrived.reshape(hit_total, 3 * tile_pix),
            (((0,), (0,)), ((), ())),
            precision=highest,
            preferred_element_type=jnp.float32,
        )

    def binning(stream, partial):
        touched = bin_call(block_slot.reshape(-1), offsets, stream, cosine, sine, hit_total, tile_pix, slot_count)
        arrived, total = exchange(touched.reshape(shards, slot_count * 3 * tile_pix), partial)
        return owner_sum(arrived, owner_flat, owner_index), total

    def projection(field, partial):
        outgoing = jnp.dot(
            (owner_flat[:, None] == jnp.arange(tiles_dev, dtype=jnp.int32)[None, :]).astype(
                jnp.float32
            ),
            field,
            precision=highest,
            preferred_element_type=jnp.float32,
        )
        touched, total = exchange(outgoing.reshape(shards, slot_count * 3 * tile_pix), partial)
        stream = read_call(
            block_slot.reshape(-1), touched.reshape(hit_total, 3 * tile_pix), offsets, cosine, sine
        )
        return stream.reshape(det_count, samp_count), total

    touched = bin_call(block_slot.reshape(-1), offsets, weigh(tod), cosine, sine, hit_total, tile_pix, slot_count)
    arrived, _, owner_lists = exchange(
        touched.reshape(shards, slot_count * 3 * tile_pix), None, hits
    )
    owner_flat = owner_lists.reshape(-1)
    owner_index = jnp.clip(owner_flat, 0, tiles_dev - 1)
    rhs = owner_sum(arrived, owner_flat, owner_index)
    solution = jnp.zeros_like(rhs)
    residual = rhs
    zeta = precondition(residual, precond)
    direction = zeta
    stream_dir, norm_now = projection(zeta, jnp.sum(residual * zeta))
    for step in range(ITERS):
        weighed = weigh(stream_dir)
        image, curvature = binning(weighed, jnp.sum(stream_dir * weighed))
        alpha = norm_now / curvature
        solution = solution + alpha * direction
        residual = residual - alpha * image
        if step + 1 < ITERS:
            zeta = precondition(residual, precond)
            stream_zeta, norm_next = projection(zeta, jnp.sum(residual * zeta))
            beta = norm_next / norm_now
            direction = zeta + beta * direction
            stream_dir = stream_zeta + beta * stream_dir
            norm_now = norm_next
    return (solution.reshape(tiles_dev, 3, tile_pix), residual.reshape(tiles_dev, 3, tile_pix))


def solution(mesh):
    in_specs = (
        P("map", "tod"),
        P("map"),
        P("map", "tod"),
        P("map", "tod"),
        P("map", "tod"),
        P(("tod", "map"), None, None),
        P("map", None),
        P(("tod", "map"), None, None),
    )
    out_specs = (P(("tod", "map"), None, None), P(("tod", "map"), None, None))
    return jax.shard_map(local, mesh=mesh, in_specs=in_specs, out_specs=out_specs, check_vma=False)
```

```python
import functools

import jax
import jax.numpy as jnp
from jax import lax
from jax.experimental import pallas as pl
from jax.experimental.pallas import tpu as pltpu
from jax.sharding import PartitionSpec as P

ANGLES = 64
ITERS = 2
SIDE = 128


def extended(cells, sides, width):
    for axis, dim in sides:
        count = lax.axis_size(axis)
        ends = count - 1
        head = lax.slice_in_dim(cells, 0, width, axis=dim)
        tail = lax.slice_in_dim(cells, cells.shape[dim] - width, cells.shape[dim], axis=dim)
        cells = jnp.concatenate(
            [
                lax.ppermute(tail, axis, [(i, (i + 1) % count) for i in range(ends)]),
                cells,
                lax.ppermute(head, axis, [((i + 1) % count, i) for i in range(ends)]),
            ],
            axis=dim,
        )
    return cells


def precondition(field, precond):
    tile = precond.shape[2]
    first, second, third = (field[:, 0:tile], field[:, tile : 2 * tile], field[:, 2 * tile :])
    row_one = precond[:, 0] * first + precond[:, 3] * second + precond[:, 4] * third
    row_two = precond[:, 3] * first + precond[:, 1] * second + precond[:, 5] * third
    row_three = precond[:, 4] * first + precond[:, 5] * second + precond[:, 2] * third
    return jnp.concatenate([row_one, row_two, row_three], axis=1)


def exchange(rows, partial, lists=None):
    shards = rows.shape[0]
    lane = jnp.arange(SIDE, dtype=jnp.int32)[None, :]
    extra = jnp.zeros((shards, SIDE), jnp.float32)
    if partial is not None:
        extra = jnp.where(lane == 0, partial.astype(jnp.float32), extra)
    if lists is not None:
        for k in range(lists.shape[1]):
            extra = jnp.where(lane == 1 + k, lists[:, k : k + 1].astype(jnp.float32), extra)
    rows = jnp.concatenate([rows, extra], axis=1)
    got = lax.all_to_all(rows, ("tod", "map"), split_axis=0, concat_axis=0, tiled=True)
    width = got.shape[1] - SIDE
    total = jnp.sum(got[:, width])
    if lists is None:
        return got[:, :width], total
    arrived_lists = jnp.round(got[:, width + 1 : width + 1 + lists.shape[1]]).astype(jnp.int32)
    return got[:, :width], total, arrived_lists


GROUP = 8


def bin_kernel(slot_ref, offs_ref, y_ref, cos_ref, sin_ref, out_ref, *, slots):
    dets, samples = y_ref.shape
    blocks = slot_ref.shape[0] // dets
    tile = samples // blocks
    out_ref[...] = jnp.zeros(out_ref.shape, out_ref.dtype)
    half = tile // 2
    pix = lax.broadcasted_iota(jnp.int32, (half, tile), 0)

    for first in range(0, dets, GROUP):
        def body(blk, carry):
            start = pl.multiple_of(blk * tile, tile)
            cols = pl.ds(start, tile)
            y = y_ref[first : first + GROUP, cols]
            offs = offs_ref[first : first + GROUP, cols]
            parts = [y, cos_ref[first : first + GROUP, cols] * y, sin_ref[first : first + GROUP, cols] * y]
            values = jnp.concatenate(parts, axis=0)
            high = values.astype(jnp.bfloat16)
            rest = values - high.astype(jnp.float32)
            mid = rest.astype(jnp.bfloat16)
            low = (rest - mid.astype(jnp.float32)).astype(jnp.bfloat16)
            zero = jnp.zeros((1, tile), jnp.bfloat16)
            for i in range(GROUP):
                upper = offs[i : i + 1] >= half
                pieces = [piece[s * GROUP + i : s * GROUP + i + 1] for piece in (high, mid, low) for s in range(3)]
                stack = jnp.concatenate(
                    [jnp.where(upper, zero, r) for r in pieces]
                    + [jnp.where(upper, r, zero) for r in pieces]
                    + [jnp.zeros((32 - 18, tile), jnp.bfloat16)],
                    axis=0,
                )
                hot = ((offs[i : i + 1] % half) == pix).astype(jnp.bfloat16)
                res = lax.dot_general(
                    stack, hot, (((1,), (1,)), ((), ())), preferred_element_type=jnp.float32
                )
                below = res[0:3] + res[3:6] + res[6:9]
                above = res[9:12] + res[12:15] + res[15:18]
                total = jnp.concatenate([below, above], axis=1)
                h = slot_ref[(first + i) * blocks + blk]
                row = h // slots
                lane = pl.multiple_of((h % slots) * (3 * tile), 128)
                for s in range(3):
                    spot = (pl.ds(row, 1), pl.ds(lane + s * tile, tile))
                    out_ref[spot] = out_ref[spot] + total[s : s + 1]
            return carry

        lax.fori_loop(0, blocks, body, 0)


def bin_call(slot_ids, offs, y, cos, sin, hit_total, tile, slots):
    return pl.pallas_call(
        functools.partial(bin_kernel, slots=slots),
        out_shape=jax.ShapeDtypeStruct((hit_total // slots, slots * 3 * tile), jnp.float32),
        grid_spec=pltpu.PrefetchScalarGridSpec(
            num_scalar_prefetch=1,
            grid=(1,),
            in_specs=[pl.BlockSpec(memory_space=pltpu.VMEM)] * 4,
            out_specs=pl.BlockSpec(memory_space=pltpu.VMEM),
        ),
    )(slot_ids, offs, y, cos, sin)


READ_GROUP = 16


def read_kernel(slot_ref, maps_ref, offs_ref, cos_ref, sin_ref, out_ref):
    lanes = 128
    dets, samples = offs_ref.shape
    blocks = slot_ref.shape[0] // dets
    tile = maps_ref.shape[1] // 3

    for first in range(0, dets, READ_GROUP):
        def body(blk, carry):
            rows = jnp.concatenate(
                [maps_ref[pl.ds(slot_ref[(first + i) * blocks + blk], 1), :] for i in range(READ_GROUP)],
                axis=0,
            )
            for j in range(tile // lanes):
                start = pl.multiple_of(blk * tile + j * lanes, lanes)
                cols = pl.ds(start, lanes)
                idx = offs_ref[first : first + READ_GROUP, cols]
                low = idx % lanes
                upper = idx >= lanes
                picked = []
                for s in range(3):
                    a = jnp.take_along_axis(
                        rows[:, s * tile : s * tile + lanes], low, axis=1, mode="promise_in_bounds"
                    )
                    b = jnp.take_along_axis(
                        rows[:, s * tile + lanes : (s + 1) * tile], low, axis=1, mode="promise_in_bounds"
                    )
                    picked.append(jnp.where(upper, b, a))
                c = cos_ref[first : first + READ_GROUP, cols]
                sn = sin_ref[first : first + READ_GROUP, cols]
                out_ref[first : first + READ_GROUP, cols] = picked[0] + c * picked[1] + sn * picked[2]
            return carry

        lax.fori_loop(0, blocks, body, 0)


def read_call(slots, maps, offs, cos, sin):
    return pl.pallas_call(
        read_kernel,
        out_shape=jax.ShapeDtypeStruct(offs.shape, jnp.float32),
        grid_spec=pltpu.PrefetchScalarGridSpec(
            num_scalar_prefetch=1,
            grid=(1,),
            in_specs=[pl.BlockSpec(memory_space=pltpu.VMEM)] * 4,
            out_specs=pl.BlockSpec(memory_space=pltpu.VMEM),
        ),
    )(slots, maps, offs, cos, sin)


def local(tod, det_angle, angle_index, offsets, block_slot, hit_tiles, noise_filter, precond):
    shards = lax.axis_size(("tod", "map"))
    hits = hit_tiles[0]
    slot_count = hits.shape[1]
    tiles_dev = precond.shape[0]
    tile_pix = precond.shape[2]
    det_count, samp_count = tod.shape
    blocks_per_det = block_slot.shape[1]
    block_len = samp_count // blocks_per_det
    block_total = det_count * blocks_per_det
    hit_total = shards * slot_count
    highest = lax.Precision.HIGH
    psi = det_angle[:, None] + jnp.pi * angle_index.astype(jnp.float32) / ANGLES
    cosine = jnp.cos(2.0 * psi)
    sine = jnp.sin(2.0 * psi)

    band = noise_filter.shape[1] - 1
    rows = jnp.arange(3 * band, dtype=jnp.int32)[:, None]
    cols = jnp.arange(band, dtype=jnp.int32)[None, :]
    lag = jnp.abs(rows - cols - band)
    lag_hot = (lag[:, :, None] == jnp.arange(band + 1, dtype=jnp.int32)[None, None, :]).astype(
        jnp.bfloat16
    )
    taps_high = lax.reduce_precision(noise_filter, exponent_bits=8, mantissa_bits=7)
    taps_rest = noise_filter - taps_high
    taps_mid = lax.reduce_precision(taps_rest, exponent_bits=8, mantissa_bits=7)
    taps_low = lax.reduce_precision(taps_rest - taps_mid, exponent_bits=8, mantissa_bits=7)
    toeplitz = jnp.einsum(
        "pdk,rck->pdrc",
        jnp.stack([taps_high, taps_mid, taps_low]).astype(jnp.bfloat16),
        lag_hot,
        preferred_element_type=jnp.float32,
    ).sum(axis=0)
    block_count = samp_count // band

    def weigh(stream):
        padded = extended(stream, (("tod", 1),), band).reshape(det_count, block_count + 2, band)
        stacked = jnp.concatenate(
            [padded[:, k : k + block_count] for k in range(3)], axis=2
        )
        out = jnp.einsum(
            "dbj,dji->dbi",
            stacked,
            toeplitz,
            precision=highest,
            preferred_element_type=jnp.float32,
        )
        return out.reshape(det_count, samp_count)

    def owner_sum(arrived, owner_flat, owner_index):
        placement = (
            owner_flat[:, None] == jnp.arange(tiles_dev, dtype=jnp.int32)[None, :]
        ).astype(jnp.float32)
        return lax.dot_general(
            placement,
            arrived.reshape(hit_total, 3 * tile_pix),
            (((0,), (0,)), ((), ())),
            precision=highest,
            preferred_element_type=jnp.float32,
        )

    def binning(stream, partial):
        touched = bin_call(block_slot.reshape(-1), offsets, stream, cosine, sine, hit_total, tile_pix, slot_count)
        arrived, total = exchange(touched.reshape(shards, slot_count * 3 * tile_pix), partial)
        return owner_sum(arrived, owner_flat, owner_index), total

    def projection(field, partial):
        outgoing = jnp.where(
            (owner_flat >= 0)[:, None],
            jnp.take(field, owner_index, axis=0),
            0.0,
        )
        touched, total = exchange(outgoing.reshape(shards, slot_count * 3 * tile_pix), partial)
        stream = read_call(
            block_slot.reshape(-1), touched.reshape(hit_total, 3 * tile_pix), offsets, cosine, sine
        )
        return stream.reshape(det_count, samp_count), total

    touched = bin_call(block_slot.reshape(-1), offsets, weigh(tod), cosine, sine, hit_total, tile_pix, slot_count)
    arrived, _, owner_lists = exchange(
        touched.reshape(shards, slot_count * 3 * tile_pix), None, hits
    )
    owner_flat = owner_lists.reshape(-1)
    owner_index = jnp.clip(owner_flat, 0, tiles_dev - 1)
    rhs = owner_sum(arrived, owner_flat, owner_index)
    solution = jnp.zeros_like(rhs)
    residual = rhs
    zeta = precondition(residual, precond)
    direction = zeta
    stream_dir, norm_now = projection(zeta, jnp.sum(residual * zeta))
    for step in range(ITERS):
        weighed = weigh(stream_dir)
        image, curvature = binning(weighed, jnp.sum(stream_dir * weighed))
        alpha = norm_now / curvature
        solution = solution + alpha * direction
        residual = residual - alpha * image
        if step + 1 < ITERS:
            zeta = precondition(residual, precond)
            stream_zeta, norm_next = projection(zeta, jnp.sum(residual * zeta))
            beta = norm_next / norm_now
            direction = zeta + beta * direction
            stream_dir = stream_zeta + beta * stream_dir
            norm_now = norm_next
    return (solution.reshape(tiles_dev, 3, tile_pix), residual.reshape(tiles_dev, 3, tile_pix))


def solution(mesh):
    in_specs = (
        P("map", "tod"),
        P("map"),
        P("map", "tod"),
        P("map", "tod"),
        P("map", "tod"),
        P(("tod", "map"), None, None),
        P("map", None),
        P(("tod", "map"), None, None),
    )
    out_specs = (P(("tod", "map"), None, None), P(("tod", "map"), None, None))
    return jax.shard_map(local, mesh=mesh, in_specs=in_specs, out_specs=out_specs, check_vma=False)
```
